256 devices in a mesh: dp: 64 (over y, z, core), seq: 4 (over x).
Axes of the slice: x: 4, y: 4, z: 8, core: 2. Of those that a mesh axis runs over, the one named last changes fastest.
Arguments:
- frames: bfloat16 [32768, 1536], P('dp', 'seq')
- owner_slot: int32 [32768], P('dp'), may hold values from -1 to 32767, as said below
- segment: int32 [64, 512], P('dp'), may hold values from 0 to 2, never falling along the last dimension, each value on 1 to 256 neighbouring positions
- norm_gain: float32 [1536], replicated, may hold values from 0.25 to 1.75
- expand: bfloat16 [1536, 2, 1536], P('dp', None, 'seq'), may hold values from -0.15625 to 0.15625
- kernel: float32 [9, 1536], P(None, 'seq'), may hold values from -2.5 to 2.5
- project: bfloat16 [1536, 1536], P('seq', 'dp'), may hold values from -0.15625 to 0.15625
- cotangent: bfloat16 [32768, 1536], P('dp', 'seq'), may hold values from -6 to 6
Outputs:
- output: bfloat16 [32768, 1536], P('dp', 'seq')
- grad_frames: bfloat16 [32768, 1536], P('dp', 'seq')
- grad_gain: float32 [1536], P('seq')
- grad_kernel: float32 [9, 1536], P(None, 'seq')
- grad_expand: float32 [1536, 2, 1536], P('dp', None, 'seq')
- grad_project: float32 [1536, 1536], P('seq', 'dp')
The draws below stay inside these ranges and needn't reach their ends.
Inputs may be any that keep to these rules, and one draw needn't show every extreme that they name: `owner_slot`: for each arrival row, the balanced row that takes it, or -1 for an empty arrival row; no balanced row is named twice. The live rows of each pack come first, contiguous, ordered by sending index of dp and then by arrival row; empty rows fill the pack's tail. Of the 512 arrival rows of one index of dp, at most 8 name rows of any one pack; some pack takes exactly 8 rows from every index of dp. `segment`: within each pack the utterance numbers never fall; a pack holds 3 utterances of 1 to 256 frames, one of exactly 256.
All inputs are finite; a program needn't handle non-finite values.
Results may differ from the reference program's by a relative error of at most 0.01.
Values may be sent and summed in bfloat16 or wider, within the bound.
No kernel may reach another device: no remote copies, remote signals or barrier semaphores. Data moves between devices by JAX's collectives and lax.ppermute only.
A program may use at most 128 MiB of HBM per device.

```python
import math
import jax
import jax.numpy as jnp
import numpy as np
from jax import lax

D = 1536
KSIZE = 9
USEG = 3
ROWS = 512
PACKS = 64
CAP = 8
ROWS_ALL = 32768
MOST_LEN = 256
N_SEQ = 4


def draw_frames(key, part):
    base_key, scale_key = jax.random.split(jax.random.fold_in(key, 3), 2)
    column_scale = jnp.exp(jax.random.uniform(scale_key, (1, D), jnp.float32, 0.0, math.log(10.0)))
    values = jax.random.normal(base_key, (ROWS_ALL, D), jnp.float32)
    return (0.3 * values * column_scale).astype(jnp.bfloat16)


def draw_owner_slot(key, part):
    count_key, full_key, source_key = jax.random.split(jax.random.fold_in(key, 7), 3)
    counts = jax.random.randint(count_key, (PACKS, PACKS), 0, CAP + 1)
    full_pack = jax.random.randint(full_key, (), 0, PACKS)
    counts = jnp.where(jnp.arange(PACKS)[None, :] == full_pack, CAP, counts)
    source_order = jax.vmap(lambda subkey: jax.random.permutation(subkey, ROWS))(jax.random.split(source_key, PACKS))
    bucket = source_order // CAP
    within = source_order % CAP
    sender = jnp.arange(PACKS)[:, None]
    alive_row = within < counts[sender, bucket]
    picks = (bucket[:, :, None] == jnp.arange(PACKS)[None, None, :]) & alive_row[:, :, None]
    picks = picks.astype(jnp.int32)
    before = jnp.cumsum(picks, axis=1) - picks
    rank = jnp.sum(before * picks, axis=2)
    offsets = jnp.cumsum(counts, axis=0) - counts
    landing = offsets[sender, bucket] + rank
    return jnp.where(alive_row, bucket * ROWS + landing, -1).astype(jnp.int32).reshape(ROWS_ALL)


def shard_levels(key, dims, cuts, least, top_value):
    gain, own = 1.0, jax.random.fold_in(key, 6)
    for axis_at, blocks in cuts:
        heights = jnp.exp(jax.random.uniform(jax.random.fold_in(own, axis_at), (blocks,), jnp.float32, least / len(cuts), top_value / len(cuts)))
        gain = gain * jnp.repeat(heights, dims[axis_at] // blocks).reshape([-1 if axis == axis_at else 1 for axis in range(len(dims))])
    return gain


def split_up(count, total, limit, lean):
    portions = [(1 << 20) // math.isqrt(standing ** lean) + 1 for standing in range(2, count + 1)]
    surplus, given = total - limit - (count - 1), [1] * (count - 1)
    while surplus > 0:
        free = [i for i in range(count - 1) if given[i] < limit]
        mass, budget = sum([portions[i] for i in free]), surplus
        for i in free:
            extra = min(limit - given[i], max(1, budget * portions[i] // mass), surplus)
            given[i] = given[i] + extra
            surplus = surplus - extra
    return np.array([limit] + given)


def uneven_parts(own_key, amount, total, most, skew):
    if amount == 2:
        one = jax.random.randint(own_key, (), max(1, total - most), min(most, total - 1) + 1)
        return jnp.stack([one, total - one])
    lengths = jnp.asarray(split_up(amount, total, most, skew), jnp.int32)
    pairs = (amount - 1) // 2
    giver, receiver = lengths[1:1 + 2 * pairs:2], lengths[2:2 + 2 * pairs:2]
    room = jnp.minimum(giver - 1, most - receiver)
    shifted = jax.random.randint(jax.random.fold_in(own_key, 1), (pairs,), 0, 1 << 20) % (room + 1)
    lengths = lengths.at[1:1 + 2 * pairs:2].set(giver - shifted).at[2:2 + 2 * pairs:2].set(receiver + shifted)
    return lengths[jax.random.permutation(jax.random.fold_in(own_key, 2), amount)]


def noise(stream_key, dims, deviation, reach, cuts=(), dtype=jnp.bfloat16):
    level = shard_levels(stream_key, dims, cuts, -0.22, 0.18) if cuts else 1.0
    entries = jax.random.normal(stream_key, dims, jnp.float32) * deviation * level
    return jnp.minimum(jnp.maximum(entries, -reach), reach).astype(dtype)


def setup_inputs(seed: int = 0) -> dict:
    key_of = jax.random.split(jax.random.key(seed), 9)
    return {
        "frames": draw_frames(jax.random.fold_in(key_of[8], 71), 0),
        "owner_slot": draw_owner_slot(jax.random.fold_in(key_of[8], 71), 0),
        "segment": jax.vmap(lambda own: jnp.searchsorted(jnp.cumsum(uneven_parts(own, USEG, ROWS, MOST_LEN, 2)), jnp.arange(ROWS), side="right"))(jax.random.split(key_of[2], PACKS)).reshape((PACKS, ROWS)).astype(jnp.int32),
        "norm_gain": jnp.clip(1.0 + 0.15 * jax.random.normal(key_of[3], (D,), jnp.float32), 0.25, 1.75),
        "expand": noise(key_of[4], (D, 2, D), D ** -0.5, 0.15625, ((0, 64), (2, 4))),
        "kernel": noise(key_of[5], (KSIZE, D), 5 ** -0.5, 2.5, ((1, 4),), jnp.float32),
        "project": noise(key_of[6], (D, D), D ** -0.5, 0.15625, ((0, 4), (1, 64))),
        "cotangent": noise(key_of[7], (ROWS_ALL, D), 1.0, 6.0, ((0, 64), (1, 4))),
    }


EPS = 1e-05

def conv_masks(labels):
    half_width = (KSIZE - 1) // 2
    length = labels.shape[0]
    padded = jnp.pad(labels, (half_width, half_width), constant_values=-1)
    return [(padded[tap_index:tap_index + length] == labels).astype(jnp.float32)[:, None] for tap_index in range(KSIZE)]

def depthwise(signal, kernel, tap_masks):
    half_width = (KSIZE - 1) // 2
    length = signal.shape[0]
    padded = jnp.pad(signal, ((half_width, half_width), (0, 0)))
    total = jnp.zeros(signal.shape, jnp.float32)
    for tap_index in range(KSIZE):
        total = total + kernel[tap_index] * padded[tap_index:tap_index + length] * tap_masks[tap_index]
    return total

def depthwise_back(signal, upstream, kernel, tap_masks):
    half_width = (KSIZE - 1) // 2
    length = signal.shape[0]
    padded = jnp.pad(signal, ((half_width, half_width), (0, 0)))
    spread = jnp.zeros((length + 2 * half_width, signal.shape[1]), jnp.float32)
    tap_sums = []
    for tap_index in range(KSIZE):
        masked = upstream * tap_masks[tap_index]
        tap_sums.append(lax.optimization_barrier(jnp.sum(masked * padded[tap_index:tap_index + length], axis=0)))
        spread = spread + jnp.pad(kernel[tap_index] * masked, ((tap_index, 2 * half_width - tap_index), (0, 0)))
    return (jnp.stack(tap_sums), spread[half_width:half_width + length])

def reference(frames, owner_slot, segment, norm_gain, expand, kernel, project, cotangent):
    target = jnp.where(owner_slot >= 0, owner_slot, ROWS_ALL).astype(jnp.int32)
    packed = jnp.zeros((ROWS_ALL, D), jnp.bfloat16).at[target].set(frames, mode='drop')
    live_rows = jnp.zeros((ROWS_ALL,), jnp.float32).at[target].set(1.0, mode='drop')
    quarter = D // N_SEQ
    expand_flat = expand.reshape(D, 2 * D)
    inv_root = 1.0 / math.sqrt(ROWS_ALL)

    def one_pack(totals, inputs):
        pack_rows, pack_live, labels, cot_rows = inputs
        live_col = pack_live[:, None]
        tap_masks = conv_masks(labels)
        floats = pack_rows.astype(jnp.float32)
        row_mean = lax.optimization_barrier(jnp.mean(floats, axis=1, keepdims=True))
        centred = floats - row_mean
        inv_scale = lax.rsqrt(lax.optimization_barrier(jnp.mean(centred * centred, axis=1, keepdims=True)) + EPS)
        normed = centred * inv_scale
        scaled = (normed * norm_gain).astype(jnp.bfloat16)
        joined = jnp.dot(scaled, expand_flat, preferred_element_type=jnp.float32)
        value_half = joined[:, :D]
        gate_sig = jax.nn.sigmoid(joined[:, D:])
        glu_out = value_half * gate_sig
        conv_out = depthwise(glu_out, kernel, tap_masks)
        conv_sig = jax.nn.sigmoid(conv_out)
        hidden = (conv_out * conv_sig * live_col).astype(jnp.bfloat16)
        mixed_total = jnp.zeros((ROWS, D), jnp.float32)
        for lane_pos in range(N_SEQ):
            lane_cols = slice(lane_pos * quarter, (lane_pos + 1) * quarter)
            part_out = jnp.dot(hidden[:, lane_cols], project[lane_cols], preferred_element_type=jnp.float32)
            mixed_total = mixed_total + lax.optimization_barrier(part_out.astype(jnp.bfloat16)).astype(jnp.float32)
        output = (floats + mixed_total).astype(jnp.bfloat16)
        project_term = jnp.dot(hidden.T, cot_rows, preferred_element_type=jnp.float32)
        hidden_grad = jnp.dot(cot_rows, project.T, preferred_element_type=jnp.float32) * live_col
        conv_grad = hidden_grad * (conv_sig + conv_out * conv_sig * (1.0 - conv_sig))
        kernel_term, glu_grad = depthwise_back(glu_out, conv_grad, kernel, tap_masks)
        proj_grad = jnp.stack([glu_grad * gate_sig, glu_grad * value_half * gate_sig * (1.0 - gate_sig)], axis=1).astype(jnp.bfloat16)
        expand_term = jnp.dot(scaled.T, proj_grad.reshape(ROWS, 2 * D), preferred_element_type=jnp.float32)
        scaled_grad = jnp.zeros((ROWS, D), jnp.float32)
        for lane_pos in range(N_SEQ):
            lane_cols = slice(lane_pos * quarter, (lane_pos + 1) * quarter)
            grad_block = proj_grad[:, :, lane_cols].reshape(ROWS, 2 * quarter)
            weight_block = expand[:, :, lane_cols].reshape(D, 2 * quarter)
            part_grad = jnp.dot(grad_block, weight_block.T, preferred_element_type=jnp.float32)
            scaled_grad = scaled_grad + lax.optimization_barrier(part_grad.astype(jnp.bfloat16)).astype(jnp.float32)
        normed_grad = scaled_grad * norm_gain
        first_mean = lax.optimization_barrier(jnp.mean(normed_grad, axis=1, keepdims=True))
        second_mean = lax.optimization_barrier(jnp.mean(normed_grad * normed, axis=1, keepdims=True))
        packed_grad = inv_scale * (normed_grad - first_mean - normed * second_mean) + cot_rows.astype(jnp.float32)
        gain_term = lax.optimization_barrier(jnp.sum(scaled_grad * normed, axis=0))
        totals = (totals[0] + gain_term, totals[1] + kernel_term, totals[2] + expand_term, totals[3] + project_term)
        return (totals, (output, packed_grad.astype(jnp.bfloat16)))
    start_totals = (jnp.zeros((D,), jnp.float32), jnp.zeros((KSIZE, D), jnp.float32), jnp.zeros((D, 2 * D), jnp.float32), jnp.zeros((D, D), jnp.float32))
    totals, stacked = lax.scan(one_pack, start_totals, (packed.reshape(PACKS, ROWS, D), live_rows.reshape(PACKS, ROWS), segment, cotangent.reshape(PACKS, ROWS, D)))
    output = stacked[0].reshape(ROWS_ALL, D)
    packed_grad = stacked[1].reshape(ROWS_ALL, D)
    safe_slot = jnp.maximum(owner_slot, 0).astype(jnp.int32)
    grad_frames = jnp.where((owner_slot >= 0)[:, None], packed_grad[safe_slot], jnp.zeros((), jnp.bfloat16))
    grad_gain = totals[0] * inv_root
    grad_kernel = totals[1] * inv_root
    grad_expand = totals[2].reshape(D, 2, D) * inv_root
    grad_project = totals[3] * inv_root
    return (output, grad_frames, grad_gain, grad_kernel, grad_expand, grad_project)
```

```python
import math

import jax
import jax.numpy as jnp
from jax import lax
from jax.sharding import PartitionSpec as P

D = 1536
KSIZE = 9


EPS = 1e-05


def conv_masks(labels):
    half_width = (KSIZE - 1) // 2
    length = labels.shape[0]
    padded = jnp.pad(labels, (half_width, half_width), constant_values=-1)
    return [
        (padded[tap_index : tap_index + length] == labels).astype(jnp.float32)[:, None]
        for tap_index in range(KSIZE)
    ]


def depthwise(signal, kernel, tap_masks):
    half_width = (KSIZE - 1) // 2
    length = signal.shape[0]
    padded = jnp.pad(signal, ((half_width, half_width), (0, 0)))
    total = jnp.zeros(signal.shape, jnp.float32)
    for tap_index in range(KSIZE):
        total = (
            total
            + kernel[tap_index] * padded[tap_index : tap_index + length] * tap_masks[tap_index]
        )
    return total


def depthwise_back(signal, upstream, kernel, tap_masks):
    half_width = (KSIZE - 1) // 2
    length = signal.shape[0]
    padded = jnp.pad(signal, ((half_width, half_width), (0, 0)))
    spread = jnp.zeros((length + 2 * half_width, signal.shape[1]), jnp.float32)
    tap_sums = []
    for tap_index in range(KSIZE):
        masked = upstream * tap_masks[tap_index]
        tap_sums.append(jnp.sum(masked * padded[tap_index : tap_index + length], axis=0))
        spread = spread + jnp.pad(
            kernel[tap_index] * masked, ((tap_index, 2 * half_width - tap_index), (0, 0))
        )
    return (jnp.stack(tap_sums), spread[half_width : half_width + length])


def place_rows(incoming, landing, row_count):
    flat = incoming.reshape(-1, incoming.shape[-1])
    total_slots = flat.shape[0]
    inverse = (
        jnp.full((row_count + 1,), total_slots, jnp.int32)
        .at[landing.reshape(-1)]
        .set(jnp.arange(total_slots, dtype=jnp.int32))[:row_count]
    )
    padded = jnp.concatenate([flat, jnp.zeros((1, flat.shape[1]), flat.dtype)])
    return (padded[inverse], inverse < total_slots)


def dp_bits(groups):
    return groups.bit_length() - 1


def halving_sum(blocks, groups):
    me = lax.axis_index("dp")
    bits = dp_bits(groups)
    rest = blocks.shape[1:]
    cur = blocks.reshape((2,) * bits + rest)
    axis_bits = [bits - 1 - a for a in range(bits)]
    for bit in range(bits):
        at = axis_bits.index(bit)
        mine = (me >> bit) & 1
        keep = lax.dynamic_index_in_dim(cur, mine, axis=at, keepdims=False)
        send = lax.dynamic_index_in_dim(cur, 1 - mine, axis=at, keepdims=False)
        pairs = [(i, i ^ (1 << bit)) for i in range(groups)]
        cur = keep + lax.ppermute(send, "dp", pairs)
        axis_bits.pop(at)
    return cur.reshape(rest)


def doubling_gather(shard, groups):
    me = lax.axis_index("dp")
    bits = dp_bits(groups)
    cur = shard[None]
    held = []
    for bit in reversed(range(bits)):
        pairs = [(i, i ^ (1 << bit)) for i in range(groups)]
        got = lax.ppermute(cur, "dp", pairs)
        low = (me >> bit) & 1 == 0
        cur = jnp.concatenate([jnp.where(low, cur, got), jnp.where(low, got, cur)], axis=0)
        held.insert(0, bit)
    cur = cur.reshape((2,) * bits + shard.shape)
    order = [held.index(b) for b in reversed(range(bits))]
    cur = jnp.transpose(cur, order + list(range(bits, bits + shard.ndim)))
    return cur.reshape((groups * shard.shape[0],) + shard.shape[1:])


def shards(frames, owner_slot, segment, norm_gain, expand, kernel, project, cotangent):
    row_count, quarter = frames.shape
    groups = lax.axis_size("dp")
    lane_index = lax.axis_index("seq")
    capacity = row_count // groups
    bucket_slots = groups * capacity
    dest_group = jnp.where(owner_slot >= 0, owner_slot // row_count, groups)
    onehot = (dest_group[:, None] == jnp.arange(groups, dtype=jnp.int32)[None, :]).astype(jnp.int32)
    earlier = jnp.cumsum(onehot, axis=0) - onehot
    within = jnp.sum(earlier * onehot, axis=1)
    send_pos = jnp.where(owner_slot >= 0, dest_group * capacity + within, bucket_slots)
    source_row = (
        jnp.full((bucket_slots + 1,), row_count, jnp.int32)
        .at[send_pos]
        .set(jnp.arange(row_count, dtype=jnp.int32))[:bucket_slots]
    )
    slot_padded = jnp.concatenate([owner_slot, jnp.full((1,), -1, jnp.int32)])
    named_slot = slot_padded[source_row]
    landing_out = jnp.where(named_slot >= 0, named_slot % row_count, row_count).reshape(
        groups, capacity
    )
    padded_in = jnp.concatenate([frames, jnp.zeros((1, quarter), jnp.bfloat16)])
    outgoing = padded_in[source_row].reshape(groups, capacity, quarter)
    incoming, landing = (
        lax.all_to_all(outgoing, "dp", split_axis=0, concat_axis=0, tiled=True),
        lax.all_to_all(landing_out, "dp", split_axis=0, concat_axis=0, tiled=True),
    )
    local_rows, occupied = place_rows(incoming, landing, row_count)
    whole_rows = lax.all_gather(local_rows, "seq", axis=1, tiled=True)
    live_col = occupied.astype(jnp.float32)[:, None]
    floats = whole_rows.astype(jnp.float32)
    row_mean = jnp.mean(floats, axis=1, keepdims=True)
    centred = floats - row_mean
    inv_scale = lax.rsqrt(jnp.mean(centred * centred, axis=1, keepdims=True) + EPS)
    normed = centred * inv_scale
    scaled = (normed * norm_gain).astype(jnp.bfloat16)
    expand_full = doubling_gather(expand, groups).reshape(D, 2 * quarter)
    project_full = doubling_gather(project.T, groups).T
    joined = jnp.dot(scaled, expand_full, preferred_element_type=jnp.float32)
    value_half = joined[:, :quarter]
    gate_sig = jax.nn.sigmoid(joined[:, quarter:])
    glu_out = value_half * gate_sig
    tap_masks = conv_masks(segment[0])
    conv_out = depthwise(glu_out, kernel, tap_masks)
    conv_sig = jax.nn.sigmoid(conv_out)
    hidden = (conv_out * conv_sig * live_col).astype(jnp.bfloat16)
    partial_out = jnp.dot(hidden, project_full, preferred_element_type=jnp.float32)
    mixed_share = lax.psum_scatter(
        partial_out.astype(jnp.bfloat16), "seq", scatter_dimension=1, tiled=True
    ).astype(jnp.float32)
    output = (local_rows.astype(jnp.float32) + mixed_share).astype(jnp.bfloat16)
    inv_root = 1.0 / math.sqrt(row_count * groups)
    cot_full = lax.all_gather(cotangent, "seq", axis=1, tiled=True)
    project_term = lax.dot_general(
        cot_full, hidden, (((0,), (0,)), ((), ())), preferred_element_type=jnp.float32
    )
    grad_project = (
        halving_sum(project_term.reshape(groups, D // groups, quarter), groups).T * inv_root
    )
    hidden_grad = (
        lax.dot_general(
            cot_full, project_full, (((1,), (1,)), ((), ())), preferred_element_type=jnp.float32
        )
        * live_col
    )
    conv_grad = hidden_grad * (conv_sig + conv_out * conv_sig * (1.0 - conv_sig))
    kernel_term, glu_grad = depthwise_back(glu_out, conv_grad, kernel, tap_masks)
    proj_grad = jnp.concatenate(
        [glu_grad * gate_sig, glu_grad * value_half * gate_sig * (1.0 - gate_sig)], axis=1
    ).astype(jnp.bfloat16)
    term_block = lax.dot_general(
        scaled, proj_grad, (((0,), (0,)), ((), ())), preferred_element_type=jnp.float32
    )
    grad_expand = (
        halving_sum(term_block.reshape(groups, expand.shape[0], 2, quarter), groups) * inv_root
    )
    scaled_part = lax.dot_general(
        proj_grad, expand_full, (((1,), (1,)), ((), ())), preferred_element_type=jnp.float32
    )
    normed_local = lax.dynamic_slice_in_dim(normed, lane_index * quarter, quarter, 1)
    scaled_grad = lax.psum(scaled_part.astype(jnp.bfloat16), "seq").astype(jnp.float32)
    normed_grad = scaled_grad * norm_gain
    first_mean = jnp.mean(normed_grad, axis=1, keepdims=True)
    second_mean = jnp.mean(normed_grad * normed, axis=1, keepdims=True)
    full_grad = inv_scale * (normed_grad - first_mean - normed * second_mean)
    packed_grad = lax.dynamic_slice_in_dim(full_grad, lane_index * quarter, quarter, 1)
    scaled_share = lax.dynamic_slice_in_dim(scaled_grad, lane_index * quarter, quarter, 1)
    gain_term = jnp.sum(scaled_share * normed_local, axis=0)
    gain_sum, kernel_sum = lax.psum((gain_term, kernel_term), "dp")
    back_rows = (packed_grad + cotangent.astype(jnp.float32)).astype(jnp.bfloat16)
    back_padded = jnp.concatenate([back_rows, jnp.zeros((1, quarter), jnp.bfloat16)])
    returning = back_padded[landing.reshape(-1)].reshape(groups, capacity, quarter)
    returned = lax.all_to_all(returning, "dp", split_axis=0, concat_axis=0, tiled=True)
    returned_flat = jnp.concatenate(
        [returned.reshape(bucket_slots, quarter), jnp.zeros((1, quarter), jnp.bfloat16)]
    )
    grad_frames = returned_flat[send_pos]
    return (
        output,
        grad_frames,
        gain_sum * inv_root,
        kernel_sum * inv_root,
        grad_expand,
        grad_project,
    )


def solution(mesh):
    placed = (
        P("dp", "seq"),
        P("dp"),
        P("dp", None),
        P(),
        P("dp", None, "seq"),
        P(None, "seq"),
        P("seq", "dp"),
        P("dp", "seq"),
    )
    return jax.shard_map(
        shards,
        mesh=mesh,
        in_specs=placed,
        out_specs=(
            P("dp", "seq"),
            P("dp", "seq"),
            P("seq"),
            P(None, "seq"),
            P("dp", None, "seq"),
            P("seq", "dp"),
        ),
        check_vma=False,
    )
```

```python
import math

import jax
import jax.numpy as jnp
from jax import lax
from jax.sharding import PartitionSpec as P

D = 1536
KSIZE = 9


EPS = 1e-05


def conv_masks(labels):
    half_width = (KSIZE - 1) // 2
    length = labels.shape[0]
    padded = jnp.pad(labels, (half_width, half_width), constant_values=-1)
    return [
        (padded[tap_index : tap_index + length] == labels).astype(jnp.float32)[:, None]
        for tap_index in range(KSIZE)
    ]


def depthwise(signal, kernel, tap_masks):
    half_width = (KSIZE - 1) // 2
    length = signal.shape[0]
    padded = jnp.pad(signal, ((half_width, half_width), (0, 0)))
    total = jnp.zeros(signal.shape, jnp.float32)
    for tap_index in range(KSIZE):
        total = (
            total
            + kernel[tap_index] * padded[tap_index : tap_index + length] * tap_masks[tap_index]
        )
    return total


def depthwise_back(signal, upstream, kernel, tap_masks):
    half_width = (KSIZE - 1) // 2
    length = signal.shape[0]
    padded = jnp.pad(signal, ((half_width, half_width), (0, 0)))
    spread = jnp.zeros((length + 2 * half_width, signal.shape[1]), jnp.float32)
    tap_sums = []
    for tap_index in range(KSIZE):
        masked = upstream * tap_masks[tap_index]
        tap_sums.append(jnp.sum(masked * padded[tap_index : tap_index + length], axis=0))
        spread = spread + jnp.pad(
            kernel[tap_index] * masked, ((tap_index, 2 * half_width - tap_index), (0, 0))
        )
    return (jnp.stack(tap_sums), spread[half_width : half_width + length])


def place_rows(incoming, landing, row_count):
    flat = incoming.reshape(-1, incoming.shape[-1])
    total_slots = flat.shape[0]
    inverse = (
        jnp.full((row_count + 1,), total_slots, jnp.int32)
        .at[landing.reshape(-1)]
        .set(jnp.arange(total_slots, dtype=jnp.int32))[:row_count]
    )
    padded = jnp.concatenate([flat, jnp.zeros((1, flat.shape[1]), flat.dtype)])
    return (padded[inverse], inverse < total_slots)


def dp_bits(groups):
    return groups.bit_length() - 1


def halving_sum(blocks, groups):
    me = lax.axis_index("dp")
    bits = dp_bits(groups)
    rest = blocks.shape[1:]
    cur = blocks.reshape((2,) * bits + rest)
    axis_bits = [bits - 1 - a for a in range(bits)]
    for bit in range(bits):
        at = axis_bits.index(bit)
        mine = (me >> bit) & 1
        keep = lax.dynamic_index_in_dim(cur, mine, axis=at, keepdims=False)
        send = lax.dynamic_index_in_dim(cur, 1 - mine, axis=at, keepdims=False)
        pairs = [(i, i ^ (1 << bit)) for i in range(groups)]
        cur = keep + lax.ppermute(send, "dp", pairs)
        axis_bits.pop(at)
    return cur.reshape(rest)


def butterfly_sum(values, groups):
    for bit in range(dp_bits(groups)):
        pairs = [(i, i ^ (1 << bit)) for i in range(groups)]
        values = values + lax.ppermute(values, "dp", pairs)
    return values


def doubling_gather(shard, groups):
    me = lax.axis_index("dp")
    bits = dp_bits(groups)
    cur = shard[None]
    held = []
    for bit in reversed(range(bits)):
        pairs = [(i, i ^ (1 << bit)) for i in range(groups)]
        got = lax.ppermute(cur, "dp", pairs)
        low = (me >> bit) & 1 == 0
        cur = jnp.concatenate([jnp.where(low, cur, got), jnp.where(low, got, cur)], axis=0)
        held.insert(0, bit)
    cur = cur.reshape((2,) * bits + shard.shape)
    order = [held.index(b) for b in reversed(range(bits))]
    cur = jnp.transpose(cur, order + list(range(bits, bits + shard.ndim)))
    return cur.reshape((groups * shard.shape[0],) + shard.shape[1:])


def shards(frames, owner_slot, segment, norm_gain, expand, kernel, project, cotangent):
    row_count, quarter = frames.shape
    groups = lax.axis_size("dp")
    lane_index = lax.axis_index("seq")
    capacity = row_count // groups
    bucket_slots = groups * capacity
    dest_group = jnp.where(owner_slot >= 0, owner_slot // row_count, groups)
    onehot = (dest_group[:, None] == jnp.arange(groups, dtype=jnp.int32)[None, :]).astype(jnp.int32)
    earlier = jnp.cumsum(onehot, axis=0) - onehot
    within = jnp.sum(earlier * onehot, axis=1)
    send_pos = jnp.where(owner_slot >= 0, dest_group * capacity + within, bucket_slots)
    source_row = (
        jnp.full((bucket_slots + 1,), row_count, jnp.int32)
        .at[send_pos]
        .set(jnp.arange(row_count, dtype=jnp.int32))[:bucket_slots]
    )
    slot_padded = jnp.concatenate([owner_slot, jnp.full((1,), -1, jnp.int32)])
    named_slot = slot_padded[source_row]
    landing_out = jnp.where(named_slot >= 0, named_slot % row_count, row_count).reshape(
        groups, capacity
    )
    padded_in = jnp.concatenate([frames, jnp.zeros((1, quarter), jnp.bfloat16)])
    outgoing = padded_in[source_row].reshape(groups, capacity, quarter)
    incoming, landing = (
        lax.all_to_all(outgoing, "dp", split_axis=0, concat_axis=0, tiled=True),
        lax.all_to_all(landing_out, "dp", split_axis=0, concat_axis=0, tiled=True),
    )
    local_rows, occupied = place_rows(incoming, landing, row_count)
    whole_rows = lax.all_gather(local_rows, "seq", axis=1, tiled=True)
    live_col = occupied.astype(jnp.float32)[:, None]
    floats = whole_rows.astype(jnp.float32)
    row_mean = jnp.mean(floats, axis=1, keepdims=True)
    centred = floats - row_mean
    inv_scale = lax.rsqrt(jnp.mean(centred * centred, axis=1, keepdims=True) + EPS)
    normed = centred * inv_scale
    scaled = (normed * norm_gain).astype(jnp.bfloat16)
    expand_full = doubling_gather(expand, groups).reshape(D, 2 * quarter)
    project_full = doubling_gather(project.T, groups).T
    joined = jnp.dot(scaled, expand_full, preferred_element_type=jnp.float32)
    value_half = joined[:, :quarter]
    gate_sig = jax.nn.sigmoid(joined[:, quarter:])
    glu_out = value_half * gate_sig
    tap_masks = conv_masks(segment[0])
    conv_out = depthwise(glu_out, kernel, tap_masks)
    conv_sig = jax.nn.sigmoid(conv_out)
    hidden = (conv_out * conv_sig * live_col).astype(jnp.bfloat16)
    partial_out = jnp.dot(hidden, project_full, preferred_element_type=jnp.float32)
    mixed_share = lax.psum_scatter(
        partial_out.astype(jnp.bfloat16), "seq", scatter_dimension=1, tiled=True
    ).astype(jnp.float32)
    output = (local_rows.astype(jnp.float32) + mixed_share).astype(jnp.bfloat16)
    inv_root = 1.0 / math.sqrt(row_count * groups)
    cot_full = lax.all_gather(cotangent, "seq", axis=1, tiled=True)
    project_term = lax.dot_general(
        cot_full, hidden, (((0,), (0,)), ((), ())), preferred_element_type=jnp.float32
    )
    grad_project = (
        halving_sum(project_term.reshape(groups, D // groups, quarter), groups).T * inv_root
    )
    hidden_grad = (
        lax.dot_general(
            cot_full, project_full, (((1,), (1,)), ((), ())), preferred_element_type=jnp.float32
        )
        * live_col
    )
    conv_grad = hidden_grad * (conv_sig + conv_out * conv_sig * (1.0 - conv_sig))
    kernel_term, glu_grad = depthwise_back(glu_out, conv_grad, kernel, tap_masks)
    proj_grad = jnp.concatenate(
        [glu_grad * gate_sig, glu_grad * value_half * gate_sig * (1.0 - gate_sig)], axis=1
    ).astype(jnp.bfloat16)
    term_block = lax.dot_general(
        scaled, proj_grad, (((0,), (0,)), ((), ())), preferred_element_type=jnp.float32
    )
    grad_expand = (
        halving_sum(term_block.reshape(groups, expand.shape[0], 2, quarter), groups) * inv_root
    )
    scaled_part = lax.dot_general(
        proj_grad, expand_full, (((1,), (1,)), ((), ())), preferred_element_type=jnp.float32
    )
    normed_local = lax.dynamic_slice_in_dim(normed, lane_index * quarter, quarter, 1)
    scaled_grad = lax.psum(scaled_part.astype(jnp.bfloat16), "seq").astype(jnp.float32)
    normed_grad = scaled_grad * norm_gain
    first_mean = jnp.mean(normed_grad, axis=1, keepdims=True)
    second_mean = jnp.mean(normed_grad * normed, axis=1, keepdims=True)
    full_grad = inv_scale * (normed_grad - first_mean - normed * second_mean)
    packed_grad = lax.dynamic_slice_in_dim(full_grad, lane_index * quarter, quarter, 1)
    scaled_share = lax.dynamic_slice_in_dim(scaled_grad, lane_index * quarter, quarter, 1)
    gain_term = jnp.sum(scaled_share * normed_local, axis=0)
    small_sums = butterfly_sum(jnp.concatenate([gain_term[None], kernel_term], axis=0), groups)
    gain_sum, kernel_sum = small_sums[0], small_sums[1:]
    back_rows = (packed_grad + cotangent.astype(jnp.float32)).astype(jnp.bfloat16)
    back_padded = jnp.concatenate([back_rows, jnp.zeros((1, quarter), jnp.bfloat16)])
    returning = back_padded[landing.reshape(-1)].reshape(groups, capacity, quarter)
    returned = lax.all_to_all(returning, "dp", split_axis=0, concat_axis=0, tiled=True)
    returned_flat = jnp.concatenate(
        [returned.reshape(bucket_slots, quarter), jnp.zeros((1, quarter), jnp.bfloat16)]
    )
    grad_frames = returned_flat[send_pos]
    return (
        output,
        grad_frames,
        gain_sum * inv_root,
        kernel_sum * inv_root,
        grad_expand,
        grad_project,
    )


def solution(mesh):
    placed = (
        P("dp", "seq"),
        P("dp"),
        P("dp", None),
        P(),
        P("dp", None, "seq"),
        P(None, "seq"),
        P("seq", "dp"),
        P("dp", "seq"),
    )
    return jax.shard_map(
        shards,
        mesh=mesh,
        in_specs=placed,
        out_specs=(
            P("dp", "seq"),
            P("dp", "seq"),
            P("seq"),
            P(None, "seq"),
            P("dp", None, "seq"),
            P("seq", "dp"),
        ),
        check_vma=False,
    )
```

```python
import math

import jax
import jax.numpy as jnp
from jax import lax
from jax.sharding import PartitionSpec as P

D = 1536
KSIZE = 9


EPS = 1e-05


def conv_masks(labels):
    half_width = (KSIZE - 1) // 2
    length = labels.shape[0]
    padded = jnp.pad(labels, (half_width, half_width), constant_values=-1)
    return [
        (padded[tap_index : tap_index + length] == labels).astype(jnp.float32)[:, None]
        for tap_index in range(KSIZE)
    ]


def depthwise(signal, kernel, tap_masks):
    half_width = (KSIZE - 1) // 2
    length = signal.shape[0]
    padded = jnp.pad(signal, ((half_width, half_width), (0, 0)))
    total = jnp.zeros(signal.shape, jnp.float32)
    for tap_index in range(KSIZE):
        total = (
            total
            + kernel[tap_index] * padded[tap_index : tap_index + length] * tap_masks[tap_index]
        )
    return total


def depthwise_back(signal, upstream, kernel, tap_masks):
    half_width = (KSIZE - 1) // 2
    length = signal.shape[0]
    padded = jnp.pad(signal, ((half_width, half_width), (0, 0)))
    spread = jnp.zeros((length + 2 * half_width, signal.shape[1]), jnp.float32)
    tap_sums = []
    for tap_index in range(KSIZE):
        masked = upstream * tap_masks[tap_index]
        tap_sums.append(jnp.sum(masked * padded[tap_index : tap_index + length], axis=0))
        spread = spread + jnp.pad(
            kernel[tap_index] * masked, ((tap_index, 2 * half_width - tap_index), (0, 0))
        )
    return (jnp.stack(tap_sums), spread[half_width : half_width + length])


def place_rows(incoming, landing, row_count):
    flat = incoming.reshape(-1, incoming.shape[-1])
    total_slots = flat.shape[0]
    inverse = (
        jnp.full((row_count + 1,), total_slots, jnp.int32)
        .at[landing.reshape(-1)]
        .set(jnp.arange(total_slots, dtype=jnp.int32))[:row_count]
    )
    padded = jnp.concatenate([flat, jnp.zeros((1, flat.shape[1]), flat.dtype)])
    return (padded[inverse], inverse < total_slots)


def dp_bits(groups):
    return groups.bit_length() - 1


def halving_sum(blocks, groups, order, wire=jnp.bfloat16):
    me = lax.axis_index("dp")
    bits = dp_bits(groups)
    rest = blocks.shape[1:]
    cur = blocks.reshape((2,) * bits + rest)
    axis_bits = [bits - 1 - a for a in range(bits)]
    for step, bit in enumerate(order):
        at = axis_bits.index(bit)
        mine = (me >> bit) & 1
        keep = lax.dynamic_index_in_dim(cur, mine, axis=at, keepdims=False)
        send = lax.dynamic_index_in_dim(cur, 1 - mine, axis=at, keepdims=False)
        if step > 0:
            send = send.astype(wire)
        pairs = [(i, i ^ (1 << bit)) for i in range(groups)]
        cur = keep + lax.ppermute(send, "dp", pairs).astype(keep.dtype)
        axis_bits.pop(at)
    return cur.reshape(rest)


def butterfly_sum(values, groups):
    for bit in range(dp_bits(groups)):
        pairs = [(i, i ^ (1 << bit)) for i in range(groups)]
        values = values + lax.ppermute(values, "dp", pairs)
    return values


def doubling_gather(shard, groups, order):
    me = lax.axis_index("dp")
    bits = dp_bits(groups)
    cur = shard[None]
    held = []
    for bit in order:
        pairs = [(i, i ^ (1 << bit)) for i in range(groups)]
        got = lax.ppermute(cur, "dp", pairs)
        low = (me >> bit) & 1 == 0
        cur = jnp.concatenate([jnp.where(low, cur, got), jnp.where(low, got, cur)], axis=0)
        held.insert(0, bit)
    cur = cur.reshape((2,) * bits + shard.shape)
    axes = [held.index(b) for b in reversed(range(bits))]
    cur = jnp.transpose(cur, axes + list(range(bits, bits + shard.ndim)))
    return cur.reshape((groups * shard.shape[0],) + shard.shape[1:])


def link_orders(groups):
    bits = dp_bits(groups)
    z_bits = list(range(1, min(4, bits)))
    y_bits = list(range(4, bits))
    return [0] + z_bits + y_bits, [0] + y_bits + z_bits


def shards(frames, owner_slot, segment, norm_gain, expand, kernel, project, cotangent):
    row_count, quarter = frames.shape
    groups = lax.axis_size("dp")
    lane_index = lax.axis_index("seq")
    capacity = row_count // groups
    bucket_slots = groups * capacity
    dest_group = jnp.where(owner_slot >= 0, owner_slot // row_count, groups)
    onehot = (dest_group[:, None] == jnp.arange(groups, dtype=jnp.int32)[None, :]).astype(jnp.int32)
    earlier = jnp.cumsum(onehot, axis=0) - onehot
    within = jnp.sum(earlier * onehot, axis=1)
    send_pos = jnp.where(owner_slot >= 0, dest_group * capacity + within, bucket_slots)
    source_row = (
        jnp.full((bucket_slots + 1,), row_count, jnp.int32)
        .at[send_pos]
        .set(jnp.arange(row_count, dtype=jnp.int32))[:bucket_slots]
    )
    slot_padded = jnp.concatenate([owner_slot, jnp.full((1,), -1, jnp.int32)])
    named_slot = slot_padded[source_row]
    landing_out = jnp.where(named_slot >= 0, named_slot % row_count, row_count).reshape(
        groups, capacity
    )
    padded_in = jnp.concatenate([frames, jnp.zeros((1, quarter), jnp.bfloat16)])
    outgoing = padded_in[source_row].reshape(groups, capacity, quarter)
    incoming, landing = (
        lax.all_to_all(outgoing, "dp", split_axis=0, concat_axis=0, tiled=True),
        lax.all_to_all(landing_out, "dp", split_axis=0, concat_axis=0, tiled=True),
    )
    cot_full = lax.all_gather(cotangent, "seq", axis=1, tiled=True)
    local_rows, occupied = place_rows(incoming, landing, row_count)
    cot_full, local_rows = lax.optimization_barrier((cot_full, local_rows))
    whole_rows = lax.all_gather(local_rows, "seq", axis=1, tiled=True)
    live_col = occupied.astype(jnp.float32)[:, None]
    floats = whole_rows.astype(jnp.float32)
    row_mean = jnp.mean(floats, axis=1, keepdims=True)
    centred = floats - row_mean
    inv_scale = lax.rsqrt(jnp.mean(centred * centred, axis=1, keepdims=True) + EPS)
    normed = centred * inv_scale
    scaled = (normed * norm_gain).astype(jnp.bfloat16)
    z_first, y_first = link_orders(groups)
    expand_full = doubling_gather(expand, groups, z_first[::-1]).reshape(D, 2 * quarter)
    project_full = doubling_gather(project.T, groups, y_first[::-1]).T
    joined = jnp.dot(scaled, expand_full, preferred_element_type=jnp.float32)
    value_half = joined[:, :quarter]
    gate_sig = jax.nn.sigmoid(joined[:, quarter:])
    glu_out = value_half * gate_sig
    tap_masks = conv_masks(segment[0])
    conv_out = depthwise(glu_out, kernel, tap_masks)
    conv_sig = jax.nn.sigmoid(conv_out)
    hidden = (conv_out * conv_sig * live_col).astype(jnp.bfloat16)
    partial_out = jnp.dot(hidden, project_full, preferred_element_type=jnp.float32)
    mixed_share = lax.psum_scatter(
        partial_out.astype(jnp.bfloat16), "seq", scatter_dimension=1, tiled=True
    ).astype(jnp.float32)
    output = (local_rows.astype(jnp.float32) + mixed_share).astype(jnp.bfloat16)
    inv_root = 1.0 / math.sqrt(row_count * groups)
    project_term = lax.dot_general(
        cot_full, hidden, (((0,), (0,)), ((), ())), preferred_element_type=jnp.float32
    )
    grad_project = (
        halving_sum(project_term.reshape(groups, D // groups, quarter), groups, y_first).T * inv_root
    )
    hidden_grad = (
        lax.dot_general(
            cot_full, project_full, (((1,), (1,)), ((), ())), preferred_element_type=jnp.float32
        )
        * live_col
    )
    conv_grad = hidden_grad * (conv_sig + conv_out * conv_sig * (1.0 - conv_sig))
    kernel_term, glu_grad = depthwise_back(glu_out, conv_grad, kernel, tap_masks)
    proj_grad = jnp.concatenate(
        [glu_grad * gate_sig, glu_grad * value_half * gate_sig * (1.0 - gate_sig)], axis=1
    ).astype(jnp.bfloat16)
    term_block = lax.dot_general(
        scaled, proj_grad, (((0,), (0,)), ((), ())), preferred_element_type=jnp.float32
    )
    grad_expand = (
        halving_sum(term_block.reshape(groups, expand.shape[0], 2, quarter), groups, z_first) * inv_root
    )
    scaled_part = lax.dot_general(
        proj_grad, expand_full, (((1,), (1,)), ((), ())), preferred_element_type=jnp.float32
    )
    normed_local = lax.dynamic_slice_in_dim(normed, lane_index * quarter, quarter, 1)
    scaled_grad = lax.psum(scaled_part.astype(jnp.bfloat16), "seq").astype(jnp.float32)
    normed_grad = scaled_grad * norm_gain
    first_mean = jnp.mean(normed_grad, axis=1, keepdims=True)
    second_mean = jnp.mean(normed_grad * normed, axis=1, keepdims=True)
    full_grad = inv_scale * (normed_grad - first_mean - normed * second_mean)
    packed_grad = lax.dynamic_slice_in_dim(full_grad, lane_index * quarter, quarter, 1)
    scaled_share = lax.dynamic_slice_in_dim(scaled_grad, lane_index * quarter, quarter, 1)
    gain_term = jnp.sum(scaled_share * normed_local, axis=0)
    small_sums = butterfly_sum(jnp.concatenate([gain_term[None], kernel_term], axis=0), groups)
    gain_sum, kernel_sum = small_sums[0], small_sums[1:]
    back_rows = (packed_grad + cotangent.astype(jnp.float32)).astype(jnp.bfloat16)
    back_padded = jnp.concatenate([back_rows, jnp.zeros((1, quarter), jnp.bfloat16)])
    returning = back_padded[landing.reshape(-1)].reshape(groups, capacity, quarter)
    returned = lax.all_to_all(returning, "dp", split_axis=0, concat_axis=0, tiled=True)
    returned_flat = jnp.concatenate(
        [returned.reshape(bucket_slots, quarter), jnp.zeros((1, quarter), jnp.bfloat16)]
    )
    grad_frames = returned_flat[send_pos]
    return (
        output,
        grad_frames,
        gain_sum * inv_root,
        kernel_sum * inv_root,
        grad_expand,
        grad_project,
    )


def solution(mesh):
    placed = (
        P("dp", "seq"),
        P("dp"),
        P("dp", None),
        P(),
        P("dp", None, "seq"),
        P(None, "seq"),
        P("seq", "dp"),
        P("dp", "seq"),
    )
    return jax.shard_map(
        shards,
        mesh=mesh,
        in_specs=placed,
        out_specs=(
            P("dp", "seq"),
            P("dp", "seq"),
            P("seq"),
            P(None, "seq"),
            P("dp", None, "seq"),
            P("seq", "dp"),
        ),
        check_vma=False,
    )
```

```python
import math

import jax
import jax.numpy as jnp
from jax import lax
from jax.sharding import PartitionSpec as P

D = 1536
KSIZE = 9


EPS = 1e-05


def conv_masks(labels):
    half_width = (KSIZE - 1) // 2
    length = labels.shape[0]
    padded = jnp.pad(labels, (half_width, half_width), constant_values=-1)
    return [
        (padded[tap_index : tap_index + length] == labels).astype(jnp.float32)[:, None]
        for tap_index in range(KSIZE)
    ]


def depthwise(signal, kernel, tap_masks):
    half_width = (KSIZE - 1) // 2
    length = signal.shape[0]
    padded = jnp.pad(signal, ((half_width, half_width), (0, 0)))
    total = jnp.zeros(signal.shape, jnp.float32)
    for tap_index in range(KSIZE):
        total = (
            total
            + kernel[tap_index] * padded[tap_index : tap_index + length] * tap_masks[tap_index]
        )
    return total


def depthwise_back(signal, upstream, kernel, tap_masks):
    half_width = (KSIZE - 1) // 2
    length = signal.shape[0]
    padded = jnp.pad(signal, ((half_width, half_width), (0, 0)))
    spread = jnp.zeros((length + 2 * half_width, signal.shape[1]), jnp.float32)
    tap_sums = []
    for tap_index in range(KSIZE):
        masked = upstream * tap_masks[tap_index]
        tap_sums.append(jnp.sum(masked * padded[tap_index : tap_index + length], axis=0))
        spread = spread + jnp.pad(
            kernel[tap_index] * masked, ((tap_index, 2 * half_width - tap_index), (0, 0))
        )
    return (jnp.stack(tap_sums), spread[half_width : half_width + length])


def place_rows(incoming, landing, row_count):
    flat = incoming.reshape(-1, incoming.shape[-1])
    total_slots = flat.shape[0]
    inverse = (
        jnp.full((row_count + 1,), total_slots, jnp.int32)
        .at[landing.reshape(-1)]
        .set(jnp.arange(total_slots, dtype=jnp.int32))[:row_count]
    )
    padded = jnp.concatenate([flat, jnp.zeros((1, flat.shape[1]), flat.dtype)])
    return (padded[inverse], inverse < total_slots)


def dp_bits(groups):
    return groups.bit_length() - 1


def halving_sum(blocks, groups, order, wire=jnp.bfloat16):
    me = lax.axis_index("dp")
    bits = dp_bits(groups)
    rest = blocks.shape[1:]
    cur = blocks.reshape((2,) * bits + rest)
    axis_bits = [bits - 1 - a for a in range(bits)]
    for step, bit in enumerate(order):
        at = axis_bits.index(bit)
        mine = (me >> bit) & 1
        keep = lax.dynamic_index_in_dim(cur, mine, axis=at, keepdims=False)
        send = lax.dynamic_index_in_dim(cur, 1 - mine, axis=at, keepdims=False)
        if step > 0:
            send = send.astype(wire)
        pairs = [(i, i ^ (1 << bit)) for i in range(groups)]
        cur = keep + lax.ppermute(send, "dp", pairs).astype(keep.dtype)
        axis_bits.pop(at)
    return cur.reshape(rest)


def butterfly_sum(values, groups):
    for bit in range(dp_bits(groups)):
        pairs = [(i, i ^ (1 << bit)) for i in range(groups)]
        values = values + lax.ppermute(values, "dp", pairs)
    return values


def seq_butterfly(values):
    lanes = lax.axis_size("seq")
    for bit in range(lanes.bit_length() - 1):
        pairs = [(i, i ^ (1 << bit)) for i in range(lanes)]
        values = values + lax.ppermute(values, "seq", pairs)
    return values


def doubling_gather(shard, groups, order):
    me = lax.axis_index("dp")
    bits = dp_bits(groups)
    cur = shard[None]
    held = []
    for bit in order:
        pairs = [(i, i ^ (1 << bit)) for i in range(groups)]
        got = lax.ppermute(cur, "dp", pairs)
        low = (me >> bit) & 1 == 0
        cur = jnp.concatenate([jnp.where(low, cur, got), jnp.where(low, got, cur)], axis=0)
        held.insert(0, bit)
    cur = cur.reshape((2,) * bits + shard.shape)
    axes = [held.index(b) for b in reversed(range(bits))]
    cur = jnp.transpose(cur, axes + list(range(bits, bits + shard.ndim)))
    return cur.reshape((groups * shard.shape[0],) + shard.shape[1:])


def link_orders(groups):
    bits = dp_bits(groups)
    z_bits = list(range(1, min(4, bits)))
    y_bits = list(range(4, bits))
    return [0] + z_bits + y_bits, [0] + y_bits + z_bits


def shards(frames, owner_slot, segment, norm_gain, expand, kernel, project, cotangent):
    row_count, quarter = frames.shape
    groups = lax.axis_size("dp")
    lane_index = lax.axis_index("seq")
    capacity = row_count // groups
    bucket_slots = groups * capacity
    dest_group = jnp.where(owner_slot >= 0, owner_slot // row_count, groups)
    onehot = (dest_group[:, None] == jnp.arange(groups, dtype=jnp.int32)[None, :]).astype(jnp.int32)
    earlier = jnp.cumsum(onehot, axis=0) - onehot
    within = jnp.sum(earlier * onehot, axis=1)
    send_pos = jnp.where(owner_slot >= 0, dest_group * capacity + within, bucket_slots)
    source_row = (
        jnp.full((bucket_slots + 1,), row_count, jnp.int32)
        .at[send_pos]
        .set(jnp.arange(row_count, dtype=jnp.int32))[:bucket_slots]
    )
    slot_padded = jnp.concatenate([owner_slot, jnp.full((1,), -1, jnp.int32)])
    named_slot = slot_padded[source_row]
    landing_out = jnp.where(named_slot >= 0, named_slot % row_count, row_count).reshape(
        groups, capacity
    )
    padded_in = jnp.concatenate([frames, jnp.zeros((1, quarter), jnp.bfloat16)])
    outgoing = padded_in[source_row].reshape(groups, capacity, quarter)
    incoming, landing = (
        lax.all_to_all(outgoing, "dp", split_axis=0, concat_axis=0, tiled=True),
        lax.all_to_all(landing_out, "dp", split_axis=0, concat_axis=0, tiled=True),
    )
    cot_full = lax.all_gather(cotangent, "seq", axis=1, tiled=True)
    local_rows, occupied = place_rows(incoming, landing, row_count)
    cot_full, local_rows = lax.optimization_barrier((cot_full, local_rows))
    whole_rows = lax.all_gather(local_rows, "seq", axis=1, tiled=True)
    live_col = occupied.astype(jnp.float32)[:, None]
    floats = whole_rows.astype(jnp.float32)
    row_mean = jnp.mean(floats, axis=1, keepdims=True)
    centred = floats - row_mean
    inv_scale = lax.rsqrt(jnp.mean(centred * centred, axis=1, keepdims=True) + EPS)
    normed = centred * inv_scale
    scaled = (normed * norm_gain).astype(jnp.bfloat16)
    z_first, y_first = link_orders(groups)
    block_rows = expand.shape[0]
    both = jnp.concatenate([expand.reshape(block_rows, 2 * quarter), project.T], axis=1)
    both_full = doubling_gather(both, groups, z_first[::-1])
    expand_full = both_full[:, : 2 * quarter]
    project_full = both_full[:, 2 * quarter :].T
    joined = jnp.dot(scaled, expand_full, preferred_element_type=jnp.float32)
    value_half = joined[:, :quarter]
    gate_sig = jax.nn.sigmoid(joined[:, quarter:])
    glu_out = value_half * gate_sig
    tap_masks = conv_masks(segment[0])
    conv_out = depthwise(glu_out, kernel, tap_masks)
    conv_sig = jax.nn.sigmoid(conv_out)
    hidden = (conv_out * conv_sig * live_col).astype(jnp.bfloat16)
    partial_out = jnp.dot(hidden, project_full, preferred_element_type=jnp.float32)
    mixed_share = lax.psum_scatter(
        partial_out.astype(jnp.bfloat16), "seq", scatter_dimension=1, tiled=True
    ).astype(jnp.float32)
    output = (local_rows.astype(jnp.float32) + mixed_share).astype(jnp.bfloat16)
    inv_root = 1.0 / math.sqrt(row_count * groups)
    project_term = lax.dot_general(
        cot_full, hidden, (((0,), (0,)), ((), ())), preferred_element_type=jnp.float32
    )
    grad_project = (
        halving_sum(project_term.reshape(groups, D // groups, quarter), groups, y_first).T * inv_root
    )
    hidden_grad = (
        lax.dot_general(
            cot_full, project_full, (((1,), (1,)), ((), ())), preferred_element_type=jnp.float32
        )
        * live_col
    )
    conv_grad = hidden_grad * (conv_sig + conv_out * conv_sig * (1.0 - conv_sig))
    kernel_term, glu_grad = depthwise_back(glu_out, conv_grad, kernel, tap_masks)
    proj_grad = jnp.concatenate(
        [glu_grad * gate_sig, glu_grad * value_half * gate_sig * (1.0 - gate_sig)], axis=1
    ).astype(jnp.bfloat16)
    term_block = lax.dot_general(
        scaled, proj_grad, (((0,), (0,)), ((), ())), preferred_element_type=jnp.float32
    )
    grad_expand = (
        halving_sum(term_block.reshape(groups, expand.shape[0], 2, quarter), groups, z_first) * inv_root
    )
    scaled_part = lax.dot_general(
        proj_grad, expand_full, (((1,), (1,)), ((), ())), preferred_element_type=jnp.float32
    )
    normed_local = lax.dynamic_slice_in_dim(normed, lane_index * quarter, quarter, 1)
    gain_local = lax.dynamic_slice_in_dim(norm_gain, lane_index * quarter, quarter, 0)
    scaled_share = lax.psum_scatter(
        scaled_part.astype(jnp.bfloat16), "seq", scatter_dimension=1, tiled=True
    ).astype(jnp.float32)
    normed_grad = scaled_share * gain_local
    row_sums = seq_butterfly(
        jnp.stack([jnp.sum(normed_grad, axis=1), jnp.sum(normed_grad * normed_local, axis=1)])
    )
    first_mean = row_sums[0][:, None] / D
    second_mean = row_sums[1][:, None] / D
    packed_grad = inv_scale * (normed_grad - first_mean - normed_local * second_mean)
    gain_term = jnp.sum(scaled_share * normed_local, axis=0)
    small_sums = butterfly_sum(jnp.concatenate([gain_term[None], kernel_term], axis=0), groups)
    gain_sum, kernel_sum = small_sums[0], small_sums[1:]
    back_rows = (packed_grad + cotangent.astype(jnp.float32)).astype(jnp.bfloat16)
    back_padded = jnp.concatenate([back_rows, jnp.zeros((1, quarter), jnp.bfloat16)])
    returning = back_padded[landing.reshape(-1)].reshape(groups, capacity, quarter)
    returned = lax.all_to_all(returning, "dp", split_axis=0, concat_axis=0, tiled=True)
    returned_flat = jnp.concatenate(
        [returned.reshape(bucket_slots, quarter), jnp.zeros((1, quarter), jnp.bfloat16)]
    )
    grad_frames = returned_flat[send_pos]
    return (
        output,
        grad_frames,
        gain_sum * inv_root,
        kernel_sum * inv_root,
        grad_expand,
        grad_project,
    )


def solution(mesh):
    placed = (
        P("dp", "seq"),
        P("dp"),
        P("dp", None),
        P(),
        P("dp", None, "seq"),
        P(None, "seq"),
        P("seq", "dp"),
        P("dp", "seq"),
    )
    return jax.shard_map(
        shards,
        mesh=mesh,
        in_specs=placed,
        out_specs=(
            P("dp", "seq"),
            P("dp", "seq"),
            P("seq"),
            P(None, "seq"),
            P("dp", None, "seq"),
            P("seq", "dp"),
        ),
        check_vma=False,
    )
```

```python
import math

import jax
import jax.numpy as jnp
from jax import lax
from jax.sharding import PartitionSpec as P

D = 1536
KSIZE = 9


EPS = 1e-05


def conv_masks(labels):
    half_width = (KSIZE - 1) // 2
    length = labels.shape[0]
    padded = jnp.pad(labels, (half_width, half_width), constant_values=-1)
    return [
        (padded[tap_index : tap_index + length] == labels).astype(jnp.float32)[:, None]
        for tap_index in range(KSIZE)
    ]


def depthwise(signal, kernel, tap_masks):
    half_width = (KSIZE - 1) // 2
    length = signal.shape[0]
    padded = jnp.pad(signal, ((half_width, half_width), (0, 0)))
    total = jnp.zeros(signal.shape, jnp.float32)
    for tap_index in range(KSIZE):
        total = (
            total
            + kernel[tap_index] * padded[tap_index : tap_index + length] * tap_masks[tap_index]
        )
    return total


def depthwise_back(signal, upstream, kernel, tap_masks):
    half_width = (KSIZE - 1) // 2
    length = signal.shape[0]
    padded = jnp.pad(signal, ((half_width, half_width), (0, 0)))
    spread = jnp.zeros((length + 2 * half_width, signal.shape[1]), jnp.float32)
    tap_sums = []
    for tap_index in range(KSIZE):
        masked = upstream * tap_masks[tap_index]
        tap_sums.append(jnp.sum(masked * padded[tap_index : tap_index + length], axis=0))
        spread = spread + jnp.pad(
            kernel[tap_index] * masked, ((tap_index, 2 * half_width - tap_index), (0, 0))
        )
    return (jnp.stack(tap_sums), spread[half_width : half_width + length])


def place_rows(incoming, landing, row_count):
    flat = incoming.reshape(-1, incoming.shape[-1])
    total_slots = flat.shape[0]
    inverse = (
        jnp.full((row_count + 1,), total_slots, jnp.int32)
        .at[landing.reshape(-1)]
        .set(jnp.arange(total_slots, dtype=jnp.int32))[:row_count]
    )
    padded = jnp.concatenate([flat, jnp.zeros((1, flat.shape[1]), flat.dtype)])
    return (padded[inverse], inverse < total_slots)


def dp_bits(groups):
    return groups.bit_length() - 1


def halving_sum(blocks, groups, order, wire=jnp.bfloat16):
    me = lax.axis_index("dp")
    bits = dp_bits(groups)
    rest = blocks.shape[1:]
    cur = blocks.reshape((2,) * bits + rest)
    axis_bits = [bits - 1 - a for a in range(bits)]
    for step, bit in enumerate(order):
        at = axis_bits.index(bit)
        mine = (me >> bit) & 1
        keep = lax.dynamic_index_in_dim(cur, mine, axis=at, keepdims=False)
        send = lax.dynamic_index_in_dim(cur, 1 - mine, axis=at, keepdims=False)
        if step > 0:
            send = send.astype(wire)
        pairs = [(i, i ^ (1 << bit)) for i in range(groups)]
        cur = keep + lax.ppermute(send, "dp", pairs).astype(keep.dtype)
        axis_bits.pop(at)
    return cur.reshape(rest)


def butterfly_sum(values, groups):
    for bit in range(dp_bits(groups)):
        pairs = [(i, i ^ (1 << bit)) for i in range(groups)]
        values = values + lax.ppermute(values, "dp", pairs)
    return values


def seq_butterfly(values):
    lanes = lax.axis_size("seq")
    for bit in range(lanes.bit_length() - 1):
        pairs = [(i, i ^ (1 << bit)) for i in range(lanes)]
        values = values + lax.ppermute(values, "seq", pairs)
    return values


def doubling_gather(shard, groups, order):
    me = lax.axis_index("dp")
    bits = dp_bits(groups)
    cur = shard[None]
    held = []
    for bit in order:
        pairs = [(i, i ^ (1 << bit)) for i in range(groups)]
        got = lax.ppermute(cur, "dp", pairs)
        low = (me >> bit) & 1 == 0
        cur = jnp.concatenate([jnp.where(low, cur, got), jnp.where(low, got, cur)], axis=0)
        held.insert(0, bit)
    cur = cur.reshape((2,) * bits + shard.shape)
    axes = [held.index(b) for b in reversed(range(bits))]
    cur = jnp.transpose(cur, axes + list(range(bits, bits + shard.ndim)))
    return cur.reshape((groups * shard.shape[0],) + shard.shape[1:])


def link_orders(groups):
    bits = dp_bits(groups)
    z_bits = list(range(1, min(4, bits)))
    y_bits = list(range(4, bits))
    return [0] + z_bits + y_bits, [0] + y_bits + z_bits


def shards(frames, owner_slot, segment, norm_gain, expand, kernel, project, cotangent):
    row_count, quarter = frames.shape
    groups = lax.axis_size("dp")
    lane_index = lax.axis_index("seq")
    capacity = row_count // groups
    bucket_slots = groups * capacity
    dest_group = jnp.where(owner_slot >= 0, owner_slot // row_count, groups)
    onehot = (dest_group[:, None] == jnp.arange(groups, dtype=jnp.int32)[None, :]).astype(jnp.int32)
    earlier = jnp.cumsum(onehot, axis=0) - onehot
    within = jnp.sum(earlier * onehot, axis=1)
    send_pos = jnp.where(owner_slot >= 0, dest_group * capacity + within, bucket_slots)
    source_row = (
        jnp.full((bucket_slots + 1,), row_count, jnp.int32)
        .at[send_pos]
        .set(jnp.arange(row_count, dtype=jnp.int32))[:bucket_slots]
    )
    slot_padded = jnp.concatenate([owner_slot, jnp.full((1,), -1, jnp.int32)])
    named_slot = slot_padded[source_row]
    landing_out = jnp.where(named_slot >= 0, named_slot % row_count, row_count).reshape(
        groups, capacity
    )
    padded_in = jnp.concatenate([frames, jnp.zeros((1, quarter), jnp.bfloat16)])
    outgoing = padded_in[source_row].reshape(groups, capacity, quarter)
    incoming, landing = (
        lax.all_to_all(outgoing, "dp", split_axis=0, concat_axis=0, tiled=True),
        lax.all_to_all(landing_out, "dp", split_axis=0, concat_axis=0, tiled=True),
    )
    cot_full = lax.all_gather(cotangent, "seq", axis=1, tiled=True)
    local_rows, occupied = place_rows(incoming, landing, row_count)
    cot_full, local_rows = lax.optimization_barrier((cot_full, local_rows))
    whole_rows = lax.all_gather(local_rows, "seq", axis=1, tiled=True)
    live_col = occupied.astype(jnp.float32)[:, None]
    floats = whole_rows.astype(jnp.float32)
    row_mean = jnp.mean(floats, axis=1, keepdims=True)
    centred = floats - row_mean
    inv_scale = lax.rsqrt(jnp.mean(centred * centred, axis=1, keepdims=True) + EPS)
    normed = centred * inv_scale
    scaled = (normed * norm_gain).astype(jnp.bfloat16)
    z_first, y_first = link_orders(groups)
    block_rows = expand.shape[0]
    both = jnp.concatenate([expand.reshape(block_rows, 2 * quarter), project.T], axis=1)
    both, local_rows = lax.optimization_barrier((both, local_rows))
    both_full = doubling_gather(both, groups, z_first[::-1])
    expand_full = both_full[:, : 2 * quarter]
    project_full = both_full[:, 2 * quarter :].T
    joined = jnp.dot(scaled, expand_full, preferred_element_type=jnp.float32)
    value_half = joined[:, :quarter]
    gate_sig = jax.nn.sigmoid(joined[:, quarter:])
    glu_out = value_half * gate_sig
    tap_masks = conv_masks(segment[0])
    conv_out = depthwise(glu_out, kernel, tap_masks)
    conv_sig = jax.nn.sigmoid(conv_out)
    hidden = (conv_out * conv_sig * live_col).astype(jnp.bfloat16)
    partial_out = jnp.dot(hidden, project_full, preferred_element_type=jnp.float32)
    mixed_share = lax.psum_scatter(
        partial_out.astype(jnp.bfloat16), "seq", scatter_dimension=1, tiled=True
    ).astype(jnp.float32)
    output = (local_rows.astype(jnp.float32) + mixed_share).astype(jnp.bfloat16)
    inv_root = 1.0 / math.sqrt(row_count * groups)
    project_term = lax.dot_general(
        cot_full, hidden, (((0,), (0,)), ((), ())), preferred_element_type=jnp.float32
    )
    grad_project = (
        halving_sum(project_term.reshape(groups, D // groups, quarter), groups, y_first).T * inv_root
    )
    hidden_grad = (
        lax.dot_general(
            cot_full, project_full, (((1,), (1,)), ((), ())), preferred_element_type=jnp.float32
        )
        * live_col
    )
    conv_grad = hidden_grad * (conv_sig + conv_out * conv_sig * (1.0 - conv_sig))
    kernel_term, glu_grad = depthwise_back(glu_out, conv_grad, kernel, tap_masks)
    proj_grad = jnp.concatenate(
        [glu_grad * gate_sig, glu_grad * value_half * gate_sig * (1.0 - gate_sig)], axis=1
    ).astype(jnp.bfloat16)
    term_block = lax.dot_general(
        scaled, proj_grad, (((0,), (0,)), ((), ())), preferred_element_type=jnp.float32
    )
    grad_expand = (
        halving_sum(term_block.reshape(groups, expand.shape[0], 2, quarter), groups, z_first) * inv_root
    )
    scaled_part = lax.dot_general(
        proj_grad, expand_full, (((1,), (1,)), ((), ())), preferred_element_type=jnp.float32
    )
    normed_local = lax.dynamic_slice_in_dim(normed, lane_index * quarter, quarter, 1)
    gain_local = lax.dynamic_slice_in_dim(norm_gain, lane_index * quarter, quarter, 0)
    scaled_share = lax.psum_scatter(
        scaled_part.astype(jnp.bfloat16), "seq", scatter_dimension=1, tiled=True
    ).astype(jnp.float32)
    normed_grad = scaled_share * gain_local
    row_sums = seq_butterfly(
        jnp.stack([jnp.sum(normed_grad, axis=1), jnp.sum(normed_grad * normed_local, axis=1)])
    )
    first_mean = row_sums[0][:, None] / D
    second_mean = row_sums[1][:, None] / D
    packed_grad = inv_scale * (normed_grad - first_mean - normed_local * second_mean)
    gain_term = jnp.sum(scaled_share * normed_local, axis=0)
    small_sums = butterfly_sum(jnp.concatenate([gain_term[None], kernel_term], axis=0), groups)
    gain_sum, kernel_sum = small_sums[0], small_sums[1:]
    back_rows = (packed_grad + cotangent.astype(jnp.float32)).astype(jnp.bfloat16)
    back_padded = jnp.concatenate([back_rows, jnp.zeros((1, quarter), jnp.bfloat16)])
    returning = back_padded[landing.reshape(-1)].reshape(groups, capacity, quarter)
    returned = lax.all_to_all(returning, "dp", split_axis=0, concat_axis=0, tiled=True)
    returned_flat = jnp.concatenate(
        [returned.reshape(bucket_slots, quarter), jnp.zeros((1, quarter), jnp.bfloat16)]
    )
    grad_frames = returned_flat[send_pos]
    return (
        output,
        grad_frames,
        gain_sum * inv_root,
        kernel_sum * inv_root,
        grad_expand,
        grad_project,
    )


def solution(mesh):
    placed = (
        P("dp", "seq"),
        P("dp"),
        P("dp", None),
        P(),
        P("dp", None, "seq"),
        P(None, "seq"),
        P("seq", "dp"),
        P("dp", "seq"),
    )
    return jax.shard_map(
        shards,
        mesh=mesh,
        in_specs=placed,
        out_specs=(
            P("dp", "seq"),
            P("dp", "seq"),
            P("seq"),
            P(None, "seq"),
            P("dp", None, "seq"),
            P("seq", "dp"),
        ),
        check_vma=False,
    )
```

```python
import math

import jax
import jax.numpy as jnp
from jax import lax
from jax.sharding import PartitionSpec as P

D = 1536
KSIZE = 9


EPS = 1e-05


def conv_masks(labels):
    half_width = (KSIZE - 1) // 2
    length = labels.shape[0]
    padded = jnp.pad(labels, (half_width, half_width), constant_values=-1)
    return [
        (padded[tap_index : tap_index + length] == labels).astype(jnp.float32)[:, None]
        for tap_index in range(KSIZE)
    ]


def depthwise(signal, kernel, tap_masks):
    half_width = (KSIZE - 1) // 2
    length = signal.shape[0]
    padded = jnp.pad(signal, ((half_width, half_width), (0, 0)))
    total = jnp.zeros(signal.shape, jnp.float32)
    for tap_index in range(KSIZE):
        total = (
            total
            + kernel[tap_index] * padded[tap_index : tap_index + length] * tap_masks[tap_index]
        )
    return total


def depthwise_back(signal, upstream, kernel, tap_masks):
    half_width = (KSIZE - 1) // 2
    length = signal.shape[0]
    padded = jnp.pad(signal, ((half_width, half_width), (0, 0)))
    spread = jnp.zeros((length + 2 * half_width, signal.shape[1]), jnp.float32)
    tap_sums = []
    for tap_index in range(KSIZE):
        masked = upstream * tap_masks[tap_index]
        tap_sums.append(jnp.sum(masked * padded[tap_index : tap_index + length], axis=0))
        spread = spread + jnp.pad(
            kernel[tap_index] * masked, ((tap_index, 2 * half_width - tap_index), (0, 0))
        )
    return (jnp.stack(tap_sums), spread[half_width : half_width + length])


def place_rows(incoming, landing, row_count):
    flat = incoming.reshape(-1, incoming.shape[-1])
    total_slots = flat.shape[0]
    inverse = (
        jnp.full((row_count + 1,), total_slots, jnp.int32)
        .at[landing.reshape(-1)]
        .set(jnp.arange(total_slots, dtype=jnp.int32))[:row_count]
    )
    padded = jnp.concatenate([flat, jnp.zeros((1, flat.shape[1]), flat.dtype)])
    return (padded[inverse], inverse < total_slots)


def dp_bits(groups):
    return groups.bit_length() - 1


def halving_sum(blocks, groups, order, wire=jnp.bfloat16):
    me = lax.axis_index("dp")
    bits = dp_bits(groups)
    rest = blocks.shape[1:]
    cur = blocks.reshape((2,) * bits + rest)
    axis_bits = [bits - 1 - a for a in range(bits)]
    for step, bit in enumerate(order):
        at = axis_bits.index(bit)
        mine = (me >> bit) & 1
        keep = lax.dynamic_index_in_dim(cur, mine, axis=at, keepdims=False)
        send = lax.dynamic_index_in_dim(cur, 1 - mine, axis=at, keepdims=False)
        if step > 0:
            send = send.astype(wire)
        pairs = [(i, i ^ (1 << bit)) for i in range(groups)]
        cur = keep + lax.ppermute(send, "dp", pairs).astype(keep.dtype)
        axis_bits.pop(at)
    return cur.reshape(rest)


def butterfly_sum(values, groups):
    for bit in range(dp_bits(groups)):
        pairs = [(i, i ^ (1 << bit)) for i in range(groups)]
        values = values + lax.ppermute(values, "dp", pairs)
    return values


def seq_butterfly(values):
    lanes = lax.axis_size("seq")
    for bit in range(lanes.bit_length() - 1):
        pairs = [(i, i ^ (1 << bit)) for i in range(lanes)]
        values = values + lax.ppermute(values, "seq", pairs)
    return values


def doubling_gather(shard, groups, order):
    me = lax.axis_index("dp")
    bits = dp_bits(groups)
    cur = shard[None]
    held = []
    for bit in order:
        pairs = [(i, i ^ (1 << bit)) for i in range(groups)]
        got = lax.ppermute(cur, "dp", pairs)
        low = (me >> bit) & 1 == 0
        cur = jnp.concatenate([jnp.where(low, cur, got), jnp.where(low, got, cur)], axis=0)
        held.insert(0, bit)
    cur = cur.reshape((2,) * bits + shard.shape)
    axes = [held.index(b) for b in reversed(range(bits))]
    cur = jnp.transpose(cur, axes + list(range(bits, bits + shard.ndim)))
    return cur.reshape((groups * shard.shape[0],) + shard.shape[1:])


def link_orders(groups):
    bits = dp_bits(groups)
    z_bits = list(range(1, min(4, bits)))
    y_bits = list(range(4, bits))
    return [0] + z_bits + y_bits, [0] + y_bits + z_bits


def shards(frames, owner_slot, segment, norm_gain, expand, kernel, project, cotangent):
    row_count, quarter = frames.shape
    groups = lax.axis_size("dp")
    lane_index = lax.axis_index("seq")
    capacity = row_count // groups
    bucket_slots = groups * capacity
    dest_group = jnp.where(owner_slot >= 0, owner_slot // row_count, groups)
    onehot = (dest_group[:, None] == jnp.arange(groups, dtype=jnp.int32)[None, :]).astype(jnp.int32)
    earlier = jnp.cumsum(onehot, axis=0) - onehot
    within = jnp.sum(earlier * onehot, axis=1)
    send_pos = jnp.where(owner_slot >= 0, dest_group * capacity + within, bucket_slots)
    source_row = (
        jnp.full((bucket_slots + 1,), row_count, jnp.int32)
        .at[send_pos]
        .set(jnp.arange(row_count, dtype=jnp.int32))[:bucket_slots]
    )
    slot_padded = jnp.concatenate([owner_slot, jnp.full((1,), -1, jnp.int32)])
    named_slot = slot_padded[source_row]
    landing_out = jnp.where(named_slot >= 0, named_slot % row_count, row_count).reshape(
        groups, capacity
    )
    flag_width = 128
    live_flag = jnp.broadcast_to((owner_slot >= 0).astype(jnp.bfloat16)[:, None], (row_count, flag_width))
    padded_in = jnp.concatenate(
        [jnp.concatenate([frames, live_flag], axis=1), jnp.zeros((1, quarter + flag_width), jnp.bfloat16)]
    )
    outgoing = padded_in[source_row].reshape(groups, capacity, quarter + flag_width)
    arrived = lax.all_to_all(outgoing, "dp", split_axis=0, concat_axis=0, tiled=True)
    incoming = arrived[:, :, :quarter]
    sent_count = jnp.sum((arrived[:, :, quarter] > 0.5).astype(jnp.int32), axis=1)
    first_row = jnp.cumsum(sent_count) - sent_count
    slot_rank = jnp.arange(capacity, dtype=jnp.int32)[None, :]
    landing = jnp.where(slot_rank < sent_count[:, None], first_row[:, None] + slot_rank, row_count)
    cot_full = lax.all_gather(cotangent, "seq", axis=1, tiled=True)
    local_rows, occupied = place_rows(incoming, landing, row_count)
    cot_full, local_rows = lax.optimization_barrier((cot_full, local_rows))
    whole_rows = lax.all_gather(local_rows, "seq", axis=1, tiled=True)
    live_col = occupied.astype(jnp.float32)[:, None]
    floats = whole_rows.astype(jnp.float32)
    row_mean = jnp.mean(floats, axis=1, keepdims=True)
    centred = floats - row_mean
    inv_scale = lax.rsqrt(jnp.mean(centred * centred, axis=1, keepdims=True) + EPS)
    normed = centred * inv_scale
    scaled = (normed * norm_gain).astype(jnp.bfloat16)
    z_first, y_first = link_orders(groups)
    block_rows = expand.shape[0]
    both = jnp.concatenate([expand.reshape(block_rows, 2 * quarter), project.T], axis=1)
    both_full = doubling_gather(both, groups, z_first[::-1])
    expand_full = both_full[:, : 2 * quarter]
    project_full = both_full[:, 2 * quarter :].T
    joined = jnp.dot(scaled, expand_full, preferred_element_type=jnp.float32)
    value_half = joined[:, :quarter]
    gate_sig = jax.nn.sigmoid(joined[:, quarter:])
    glu_out = value_half * gate_sig
    tap_masks = conv_masks(segment[0])
    conv_out = depthwise(glu_out, kernel, tap_masks)
    conv_sig = jax.nn.sigmoid(conv_out)
    hidden = (conv_out * conv_sig * live_col).astype(jnp.bfloat16)
    partial_out = jnp.dot(hidden, project_full, preferred_element_type=jnp.float32)
    mixed_share = lax.psum_scatter(
        partial_out.astype(jnp.bfloat16), "seq", scatter_dimension=1, tiled=True
    ).astype(jnp.float32)
    output = (local_rows.astype(jnp.float32) + mixed_share).astype(jnp.bfloat16)
    inv_root = 1.0 / math.sqrt(row_count * groups)
    project_term = lax.dot_general(
        cot_full, hidden, (((0,), (0,)), ((), ())), preferred_element_type=jnp.float32
    )
    grad_project = (
        halving_sum(project_term.reshape(groups, D // groups, quarter), groups, y_first).T * inv_root
    )
    hidden_grad = (
        lax.dot_general(
            cot_full, project_full, (((1,), (1,)), ((), ())), preferred_element_type=jnp.float32
        )
        * live_col
    )
    conv_grad = hidden_grad * (conv_sig + conv_out * conv_sig * (1.0 - conv_sig))
    kernel_term, glu_grad = depthwise_back(glu_out, conv_grad, kernel, tap_masks)
    proj_grad = jnp.concatenate(
        [glu_grad * gate_sig, glu_grad * value_half * gate_sig * (1.0 - gate_sig)], axis=1
    ).astype(jnp.bfloat16)
    term_block = lax.dot_general(
        scaled, proj_grad, (((0,), (0,)), ((), ())), preferred_element_type=jnp.float32
    )
    grad_expand = (
        halving_sum(term_block.reshape(groups, expand.shape[0], 2, quarter), groups, z_first) * inv_root
    )
    scaled_part = lax.dot_general(
        proj_grad, expand_full, (((1,), (1,)), ((), ())), preferred_element_type=jnp.float32
    )
    normed_local = lax.dynamic_slice_in_dim(normed, lane_index * quarter, quarter, 1)
    gain_local = lax.dynamic_slice_in_dim(norm_gain, lane_index * quarter, quarter, 0)
    scaled_share = lax.psum_scatter(
        scaled_part.astype(jnp.bfloat16), "seq", scatter_dimension=1, tiled=True
    ).astype(jnp.float32)
    normed_grad = scaled_share * gain_local
    row_sums = seq_butterfly(
        jnp.stack([jnp.sum(normed_grad, axis=1), jnp.sum(normed_grad * normed_local, axis=1)])
    )
    first_mean = row_sums[0][:, None] / D
    second_mean = row_sums[1][:, None] / D
    packed_grad = inv_scale * (normed_grad - first_mean - normed_local * second_mean)
    gain_term = jnp.sum(scaled_share * normed_local, axis=0)
    small_sums = butterfly_sum(jnp.concatenate([gain_term[None], kernel_term], axis=0), groups)
    gain_sum, kernel_sum = small_sums[0], small_sums[1:]
    back_rows = (packed_grad + cotangent.astype(jnp.float32)).astype(jnp.bfloat16)
    back_padded = jnp.concatenate([back_rows, jnp.zeros((1, quarter), jnp.bfloat16)])
    returning = back_padded[landing.reshape(-1)].reshape(groups, capacity, quarter)
    returned = lax.all_to_all(returning, "dp", split_axis=0, concat_axis=0, tiled=True)
    returned_flat = jnp.concatenate(
        [returned.reshape(bucket_slots, quarter), jnp.zeros((1, quarter), jnp.bfloat16)]
    )
    grad_frames = returned_flat[send_pos]
    return (
        output,
        grad_frames,
        gain_sum * inv_root,
        kernel_sum * inv_root,
        grad_expand,
        grad_project,
    )


def solution(mesh):
    placed = (
        P("dp", "seq"),
        P("dp"),
        P("dp", None),
        P(),
        P("dp", None, "seq"),
        P(None, "seq"),
        P("seq", "dp"),
        P("dp", "seq"),
    )
    return jax.shard_map(
        shards,
        mesh=mesh,
        in_specs=placed,
        out_specs=(
            P("dp", "seq"),
            P("dp", "seq"),
            P("seq"),
            P(None, "seq"),
            P("dp", None, "seq"),
            P("seq", "dp"),
        ),
        check_vma=False,
    )
```

```python
import math

import jax
import jax.numpy as jnp
from jax import lax
from jax.sharding import PartitionSpec as P

D = 1536
KSIZE = 9


EPS = 1e-05


def conv_masks(labels):
    half_width = (KSIZE - 1) // 2
    length = labels.shape[0]
    padded = jnp.pad(labels, (half_width, half_width), constant_values=-1)
    return [
        (padded[tap_index : tap_index + length] == labels).astype(jnp.float32)[:, None]
        for tap_index in range(KSIZE)
    ]


def depthwise(signal, kernel, tap_masks):
    half_width = (KSIZE - 1) // 2
    length = signal.shape[0]
    padded = jnp.pad(signal, ((half_width, half_width), (0, 0)))
    total = jnp.zeros(signal.shape, jnp.float32)
    for tap_index in range(KSIZE):
        total = (
            total
            + kernel[tap_index] * padded[tap_index : tap_index + length] * tap_masks[tap_index]
        )
    return total


def depthwise_back(signal, upstream, kernel, tap_masks):
    half_width = (KSIZE - 1) // 2
    length = signal.shape[0]
    padded = jnp.pad(signal, ((half_width, half_width), (0, 0)))
    spread = jnp.zeros((length + 2 * half_width, signal.shape[1]), jnp.float32)
    tap_sums = []
    for tap_index in range(KSIZE):
        masked = upstream * tap_masks[tap_index]
        tap_sums.append(jnp.sum(masked * padded[tap_index : tap_index + length], axis=0))
        spread = spread + jnp.pad(
            kernel[tap_index] * masked, ((tap_index, 2 * half_width - tap_index), (0, 0))
        )
    return (jnp.stack(tap_sums), spread[half_width : half_width + length])


def place_rows(incoming, landing, row_count):
    flat = incoming.reshape(-1, incoming.shape[-1])
    total_slots = flat.shape[0]
    inverse = (
        jnp.full((row_count + 1,), total_slots, jnp.int32)
        .at[landing.reshape(-1)]
        .set(jnp.arange(total_slots, dtype=jnp.int32))[:row_count]
    )
    padded = jnp.concatenate([flat, jnp.zeros((1, flat.shape[1]), flat.dtype)])
    return (padded[inverse], inverse < total_slots)


def dp_bits(groups):
    return groups.bit_length() - 1


def halving_sum(blocks, groups, order, wire=jnp.bfloat16):
    me = lax.axis_index("dp")
    bits = dp_bits(groups)
    rest = blocks.shape[1:]
    cur = blocks.reshape((2,) * bits + rest)
    axis_bits = [bits - 1 - a for a in range(bits)]
    for step, bit in enumerate(order):
        at = axis_bits.index(bit)
        mine = (me >> bit) & 1
        keep = lax.dynamic_index_in_dim(cur, mine, axis=at, keepdims=False)
        send = lax.dynamic_index_in_dim(cur, 1 - mine, axis=at, keepdims=False)
        if step > 0:
            send = send.astype(wire)
        pairs = [(i, i ^ (1 << bit)) for i in range(groups)]
        cur = keep + lax.ppermute(send, "dp", pairs).astype(keep.dtype)
        axis_bits.pop(at)
    return cur.reshape(rest)


def butterfly_sum(values, groups):
    for bit in range(dp_bits(groups)):
        pairs = [(i, i ^ (1 << bit)) for i in range(groups)]
        values = values + lax.ppermute(values, "dp", pairs)
    return values


def seq_butterfly(values):
    lanes = lax.axis_size("seq")
    for bit in range(lanes.bit_length() - 1):
        pairs = [(i, i ^ (1 << bit)) for i in range(lanes)]
        values = values + lax.ppermute(values, "seq", pairs)
    return values


def doubling_gather(shard, groups, order):
    me = lax.axis_index("dp")
    bits = dp_bits(groups)
    cur = shard[None]
    held = []
    for bit in order:
        pairs = [(i, i ^ (1 << bit)) for i in range(groups)]
        got = lax.ppermute(cur, "dp", pairs)
        low = (me >> bit) & 1 == 0
        cur = jnp.concatenate([jnp.where(low, cur, got), jnp.where(low, got, cur)], axis=0)
        held.insert(0, bit)
    cur = cur.reshape((2,) * bits + shard.shape)
    axes = [held.index(b) for b in reversed(range(bits))]
    cur = jnp.transpose(cur, axes + list(range(bits, bits + shard.ndim)))
    return cur.reshape((groups * shard.shape[0],) + shard.shape[1:])


def link_orders(groups):
    bits = dp_bits(groups)
    z_bits = list(range(1, min(4, bits)))
    y_bits = list(range(4, bits))
    return [0] + z_bits + y_bits, [0] + y_bits + z_bits


def shards(frames, owner_slot, segment, norm_gain, expand, kernel, project, cotangent):
    row_count, quarter = frames.shape
    groups = lax.axis_size("dp")
    lane_index = lax.axis_index("seq")
    capacity = row_count // groups
    bucket_slots = groups * capacity
    dest_group = jnp.where(owner_slot >= 0, owner_slot // row_count, groups)
    onehot = (dest_group[:, None] == jnp.arange(groups, dtype=jnp.int32)[None, :]).astype(jnp.int32)
    earlier = jnp.cumsum(onehot, axis=0) - onehot
    within = jnp.sum(earlier * onehot, axis=1)
    send_pos = jnp.where(owner_slot >= 0, dest_group * capacity + within, bucket_slots)
    source_row = (
        jnp.full((bucket_slots + 1,), row_count, jnp.int32)
        .at[send_pos]
        .set(jnp.arange(row_count, dtype=jnp.int32))[:bucket_slots]
    )
    slot_padded = jnp.concatenate([owner_slot, jnp.full((1,), -1, jnp.int32)])
    named_slot = slot_padded[source_row]
    landing_out = jnp.where(named_slot >= 0, named_slot % row_count, row_count).reshape(
        groups, capacity
    )
    flag_width = 128
    live_flag = jnp.broadcast_to((owner_slot >= 0).astype(jnp.bfloat16)[:, None], (row_count, flag_width))
    padded_in = jnp.concatenate(
        [jnp.concatenate([frames, live_flag], axis=1), jnp.zeros((1, quarter + flag_width), jnp.bfloat16)]
    )
    outgoing = padded_in[source_row].reshape(groups, capacity, quarter + flag_width)
    arrived = lax.all_to_all(outgoing, "dp", split_axis=0, concat_axis=0, tiled=True)
    incoming = arrived[:, :, :quarter]
    sent_count = jnp.sum((arrived[:, :, quarter] > 0.5).astype(jnp.int32), axis=1)
    first_row = jnp.cumsum(sent_count) - sent_count
    slot_rank = jnp.arange(capacity, dtype=jnp.int32)[None, :]
    landing = jnp.where(slot_rank < sent_count[:, None], first_row[:, None] + slot_rank, row_count)
    cot_full = lax.all_gather(cotangent, "seq", axis=1, tiled=True)
    local_rows, occupied = place_rows(incoming, landing, row_count)
    cot_full, local_rows = lax.optimization_barrier((cot_full, local_rows))
    whole_rows = lax.all_gather(local_rows, "seq", axis=1, tiled=True)
    live_col = occupied.astype(jnp.float32)[:, None]
    floats = whole_rows.astype(jnp.float32)
    row_mean = jnp.mean(floats, axis=1, keepdims=True)
    centred = floats - row_mean
    inv_scale = lax.rsqrt(jnp.mean(centred * centred, axis=1, keepdims=True) + EPS)
    normed = centred * inv_scale
    scaled = (normed * norm_gain).astype(jnp.bfloat16)
    z_first, y_first = link_orders(groups)
    block_rows = expand.shape[0]
    both = jnp.concatenate([expand.reshape(block_rows, 2 * quarter), project.T], axis=1)
    both_full = doubling_gather(both, groups, z_first[::-1])
    expand_full = both_full[:, : 2 * quarter]
    project_full = both_full[:, 2 * quarter :].T
    joined = jnp.dot(scaled, expand_full, preferred_element_type=jnp.float32)
    value_half = joined[:, :quarter]
    gate_sig = jax.nn.sigmoid(joined[:, quarter:])
    glu_out = value_half * gate_sig
    tap_masks = conv_masks(segment[0])
    conv_out = depthwise(glu_out, kernel, tap_masks)
    conv_sig = jax.nn.sigmoid(conv_out)
    hidden = (conv_out * conv_sig * live_col).astype(jnp.bfloat16)
    partial_out = jnp.dot(hidden, project_full, preferred_element_type=jnp.float32)
    mixed_share = lax.psum_scatter(
        partial_out.astype(jnp.bfloat16), "seq", scatter_dimension=1, tiled=True
    ).astype(jnp.float32)
    output = (local_rows.astype(jnp.float32) + mixed_share).astype(jnp.bfloat16)
    inv_root = 1.0 / math.sqrt(row_count * groups)
    project_term = lax.dot_general(
        cot_full, hidden, (((0,), (0,)), ((), ())), preferred_element_type=jnp.float32
    )
    grad_project = (
        halving_sum(project_term.reshape(groups, D // groups, quarter), groups, y_first).T * inv_root
    )
    hidden_grad = (
        lax.dot_general(
            cot_full, project_full, (((1,), (1,)), ((), ())), preferred_element_type=jnp.float32
        )
        * live_col
    )
    conv_grad = hidden_grad * (conv_sig + conv_out * conv_sig * (1.0 - conv_sig))
    kernel_term, glu_grad = depthwise_back(glu_out, conv_grad, kernel, tap_masks)
    proj_grad = jnp.concatenate(
        [glu_grad * gate_sig, glu_grad * value_half * gate_sig * (1.0 - gate_sig)], axis=1
    ).astype(jnp.bfloat16)
    term_block = lax.dot_general(
        scaled, proj_grad, (((0,), (0,)), ((), ())), preferred_element_type=jnp.float32
    )
    grad_expand = (
        halving_sum(term_block.reshape(groups, expand.shape[0], 2, quarter), groups, z_first) * inv_root
    )
    scaled_part = lax.dot_general(
        proj_grad, expand_full, (((1,), (1,)), ((), ())), preferred_element_type=jnp.float32
    )
    normed_local = lax.dynamic_slice_in_dim(normed, lane_index * quarter, quarter, 1)
    gain_local = lax.dynamic_slice_in_dim(norm_gain, lane_index * quarter, quarter, 0)
    scaled_share = lax.psum_scatter(
        scaled_part.astype(jnp.bfloat16), "seq", scatter_dimension=1, tiled=True
    ).astype(jnp.float32)
    normed_grad = scaled_share * gain_local
    row_sums = seq_butterfly(
        jnp.stack([jnp.sum(normed_grad, axis=1), jnp.sum(normed_grad * normed_local, axis=1)])
    )
    first_mean = row_sums[0][:, None] / D
    second_mean = row_sums[1][:, None] / D
    packed_grad = inv_scale * (normed_grad - first_mean - normed_local * second_mean)
    gain_term = jnp.sum(scaled_share * normed_local, axis=0)
    back_rows = (packed_grad + cotangent.astype(jnp.float32)).astype(jnp.bfloat16)
    back_padded = jnp.concatenate([back_rows, jnp.zeros((1, quarter), jnp.bfloat16)])
    returning = back_padded[landing.reshape(-1)].reshape(groups, capacity, quarter)
    small_terms = jnp.concatenate([gain_term[None], kernel_term], axis=0)
    small_terms, returning = lax.optimization_barrier((small_terms, returning))
    small_sums = butterfly_sum(small_terms, groups)
    gain_sum, kernel_sum = small_sums[0], small_sums[1:]
    returned = lax.all_to_all(returning, "dp", split_axis=0, concat_axis=0, tiled=True)
    returned_flat = jnp.concatenate(
        [returned.reshape(bucket_slots, quarter), jnp.zeros((1, quarter), jnp.bfloat16)]
    )
    grad_frames = returned_flat[send_pos]
    return (
        output,
        grad_frames,
        gain_sum * inv_root,
        kernel_sum * inv_root,
        grad_expand,
        grad_project,
    )


def solution(mesh):
    placed = (
        P("dp", "seq"),
        P("dp"),
        P("dp", None),
        P(),
        P("dp", None, "seq"),
        P(None, "seq"),
        P("seq", "dp"),
        P("dp", "seq"),
    )
    return jax.shard_map(
        shards,
        mesh=mesh,
        in_specs=placed,
        out_specs=(
            P("dp", "seq"),
            P("dp", "seq"),
            P("seq"),
            P(None, "seq"),
            P("dp", None, "seq"),
            P("seq", "dp"),
        ),
        check_vma=False,
    )
```

```python
import math

import jax
import jax.numpy as jnp
from jax import lax
from jax.sharding import PartitionSpec as P

D = 1536
KSIZE = 9


EPS = 1e-05


def conv_masks(labels):
    half_width = (KSIZE - 1) // 2
    length = labels.shape[0]
    padded = jnp.pad(labels, (half_width, half_width), constant_values=-1)
    return [
        (padded[tap_index : tap_index + length] == labels).astype(jnp.float32)[:, None]
        for tap_index in range(KSIZE)
    ]


def depthwise(signal, kernel, tap_masks):
    half_width = (KSIZE - 1) // 2
    length = signal.shape[0]
    padded = jnp.pad(signal, ((half_width, half_width), (0, 0)))
    total = jnp.zeros(signal.shape, jnp.float32)
    for tap_index in range(KSIZE):
        total = (
            total
            + kernel[tap_index] * padded[tap_index : tap_index + length] * tap_masks[tap_index]
        )
    return total


def depthwise_back(signal, upstream, kernel, tap_masks):
    half_width = (KSIZE - 1) // 2
    length = signal.shape[0]
    padded = jnp.pad(signal, ((half_width, half_width), (0, 0)))
    spread = jnp.zeros((length + 2 * half_width, signal.shape[1]), jnp.float32)
    tap_sums = []
    for tap_index in range(KSIZE):
        masked = upstream * tap_masks[tap_index]
        tap_sums.append(jnp.sum(masked * padded[tap_index : tap_index + length], axis=0))
        spread = spread + jnp.pad(
            kernel[tap_index] * masked, ((tap_index, 2 * half_width - tap_index), (0, 0))
        )
    return (jnp.stack(tap_sums), spread[half_width : half_width + length])


def place_rows(incoming, landing, row_count):
    flat = incoming.reshape(-1, incoming.shape[-1])
    total_slots = flat.shape[0]
    inverse = (
        jnp.full((row_count + 1,), total_slots, jnp.int32)
        .at[landing.reshape(-1)]
        .set(jnp.arange(total_slots, dtype=jnp.int32))[:row_count]
    )
    padded = jnp.concatenate([flat, jnp.zeros((1, flat.shape[1]), flat.dtype)])
    return (padded[inverse], inverse < total_slots)


def dp_bits(groups):
    return groups.bit_length() - 1


def halving_sum(blocks, groups, order, wire=jnp.bfloat16):
    me = lax.axis_index("dp")
    bits = dp_bits(groups)
    rest = blocks.shape[1:]
    cur = blocks.reshape((2,) * bits + rest)
    axis_bits = [bits - 1 - a for a in range(bits)]
    for step, bit in enumerate(order):
        at = axis_bits.index(bit)
        mine = (me >> bit) & 1
        keep = lax.dynamic_index_in_dim(cur, mine, axis=at, keepdims=False)
        send = lax.dynamic_index_in_dim(cur, 1 - mine, axis=at, keepdims=False)
        if step > 0:
            send = send.astype(wire)
        pairs = [(i, i ^ (1 << bit)) for i in range(groups)]
        cur = keep + lax.ppermute(send, "dp", pairs).astype(keep.dtype)
        axis_bits.pop(at)
    return cur.reshape(rest)


def butterfly_sum(values, groups):
    for bit in range(dp_bits(groups)):
        pairs = [(i, i ^ (1 << bit)) for i in range(groups)]
        values = values + lax.ppermute(values, "dp", pairs)
    return values


def seq_butterfly(values):
    lanes = lax.axis_size("seq")
    for bit in range(lanes.bit_length() - 1):
        pairs = [(i, i ^ (1 << bit)) for i in range(lanes)]
        values = values + lax.ppermute(values, "seq", pairs)
    return values


def doubling_gather(shard, groups, order, wait_for=None, wait_at=0):
    me = lax.axis_index("dp")
    bits = dp_bits(groups)
    cur = shard[None]
    held = []
    for step, bit in enumerate(order):
        if wait_for is not None and step == wait_at:
            cur, _ = lax.optimization_barrier((cur, wait_for))
        pairs = [(i, i ^ (1 << bit)) for i in range(groups)]
        got = lax.ppermute(cur, "dp", pairs)
        low = (me >> bit) & 1 == 0
        cur = jnp.concatenate([jnp.where(low, cur, got), jnp.where(low, got, cur)], axis=0)
        held.insert(0, bit)
    cur = cur.reshape((2,) * bits + shard.shape)
    axes = [held.index(b) for b in reversed(range(bits))]
    cur = jnp.transpose(cur, axes + list(range(bits, bits + shard.ndim)))
    return cur.reshape((groups * shard.shape[0],) + shard.shape[1:])


def link_orders(groups):
    bits = dp_bits(groups)
    z_bits = list(range(1, min(4, bits)))
    y_bits = list(range(4, bits))
    return [0] + z_bits + y_bits, [0] + y_bits + z_bits


def shards(frames, owner_slot, segment, norm_gain, expand, kernel, project, cotangent):
    row_count, quarter = frames.shape
    groups = lax.axis_size("dp")
    lane_index = lax.axis_index("seq")
    capacity = row_count // groups
    bucket_slots = groups * capacity
    dest_group = jnp.where(owner_slot >= 0, owner_slot // row_count, groups)
    onehot = (dest_group[:, None] == jnp.arange(groups, dtype=jnp.int32)[None, :]).astype(jnp.int32)
    earlier = jnp.cumsum(onehot, axis=0) - onehot
    within = jnp.sum(earlier * onehot, axis=1)
    send_pos = jnp.where(owner_slot >= 0, dest_group * capacity + within, bucket_slots)
    source_row = (
        jnp.full((bucket_slots + 1,), row_count, jnp.int32)
        .at[send_pos]
        .set(jnp.arange(row_count, dtype=jnp.int32))[:bucket_slots]
    )
    slot_padded = jnp.concatenate([owner_slot, jnp.full((1,), -1, jnp.int32)])
    named_slot = slot_padded[source_row]
    landing_out = jnp.where(named_slot >= 0, named_slot % row_count, row_count).reshape(
        groups, capacity
    )
    flag_width = 128
    live_flag = jnp.broadcast_to((owner_slot >= 0).astype(jnp.bfloat16)[:, None], (row_count, flag_width))
    padded_in = jnp.concatenate(
        [jnp.concatenate([frames, live_flag], axis=1), jnp.zeros((1, quarter + flag_width), jnp.bfloat16)]
    )
    outgoing = padded_in[source_row].reshape(groups, capacity, quarter + flag_width)
    arrived = lax.all_to_all(outgoing, "dp", split_axis=0, concat_axis=0, tiled=True)
    incoming = arrived[:, :, :quarter]
    sent_count = jnp.sum((arrived[:, :, quarter] > 0.5).astype(jnp.int32), axis=1)
    first_row = jnp.cumsum(sent_count) - sent_count
    slot_rank = jnp.arange(capacity, dtype=jnp.int32)[None, :]
    landing = jnp.where(slot_rank < sent_count[:, None], first_row[:, None] + slot_rank, row_count)
    cot_full = lax.all_gather(cotangent, "seq", axis=1, tiled=True)
    local_rows, occupied = place_rows(incoming, landing, row_count)
    cot_full, local_rows = lax.optimization_barrier((cot_full, local_rows))
    whole_rows = lax.all_gather(local_rows, "seq", axis=1, tiled=True)
    live_col = occupied.astype(jnp.float32)[:, None]
    floats = whole_rows.astype(jnp.float32)
    row_mean = jnp.mean(floats, axis=1, keepdims=True)
    centred = floats - row_mean
    inv_scale = lax.rsqrt(jnp.mean(centred * centred, axis=1, keepdims=True) + EPS)
    normed = centred * inv_scale
    scaled = (normed * norm_gain).astype(jnp.bfloat16)
    z_first, y_first = link_orders(groups)
    block_rows = expand.shape[0]
    both = jnp.concatenate([expand.reshape(block_rows, 2 * quarter), project.T], axis=1)
    both_full = doubling_gather(
        both, groups, z_first[::-1], wait_for=local_rows, wait_at=max(0, dp_bits(groups) - 2)
    )
    expand_full = both_full[:, : 2 * quarter]
    project_full = both_full[:, 2 * quarter :].T
    joined = jnp.dot(scaled, expand_full, preferred_element_type=jnp.float32)
    value_half = joined[:, :quarter]
    gate_sig = jax.nn.sigmoid(joined[:, quarter:])
    glu_out = value_half * gate_sig
    tap_masks = conv_masks(segment[0])
    conv_out = depthwise(glu_out, kernel, tap_masks)
    conv_sig = jax.nn.sigmoid(conv_out)
    hidden = (conv_out * conv_sig * live_col).astype(jnp.bfloat16)
    partial_out = jnp.dot(hidden, project_full, preferred_element_type=jnp.float32)
    mixed_share = lax.psum_scatter(
        partial_out.astype(jnp.bfloat16), "seq", scatter_dimension=1, tiled=True
    ).astype(jnp.float32)
    output = (local_rows.astype(jnp.float32) + mixed_share).astype(jnp.bfloat16)
    inv_root = 1.0 / math.sqrt(row_count * groups)
    project_term = lax.dot_general(
        cot_full, hidden, (((0,), (0,)), ((), ())), preferred_element_type=jnp.float32
    )
    grad_project = (
        halving_sum(project_term.reshape(groups, D // groups, quarter), groups, y_first).T * inv_root
    )
    hidden_grad = (
        lax.dot_general(
            cot_full, project_full, (((1,), (1,)), ((), ())), preferred_element_type=jnp.float32
        )
        * live_col
    )
    conv_grad = hidden_grad * (conv_sig + conv_out * conv_sig * (1.0 - conv_sig))
    kernel_term, glu_grad = depthwise_back(glu_out, conv_grad, kernel, tap_masks)
    proj_grad = jnp.concatenate(
        [glu_grad * gate_sig, glu_grad * value_half * gate_sig * (1.0 - gate_sig)], axis=1
    ).astype(jnp.bfloat16)
    term_block = lax.dot_general(
        scaled, proj_grad, (((0,), (0,)), ((), ())), preferred_element_type=jnp.float32
    )
    grad_expand = (
        halving_sum(term_block.reshape(groups, expand.shape[0], 2, quarter), groups, z_first) * inv_root
    )
    scaled_part = lax.dot_general(
        proj_grad, expand_full, (((1,), (1,)), ((), ())), preferred_element_type=jnp.float32
    )
    normed_local = lax.dynamic_slice_in_dim(normed, lane_index * quarter, quarter, 1)
    gain_local = lax.dynamic_slice_in_dim(norm_gain, lane_index * quarter, quarter, 0)
    scaled_share = lax.psum_scatter(
        scaled_part.astype(jnp.bfloat16), "seq", scatter_dimension=1, tiled=True
    ).astype(jnp.float32)
    normed_grad = scaled_share * gain_local
    row_sums = seq_butterfly(
        jnp.stack([jnp.sum(normed_grad, axis=1), jnp.sum(normed_grad * normed_local, axis=1)])
    )
    first_mean = row_sums[0][:, None] / D
    second_mean = row_sums[1][:, None] / D
    packed_grad = inv_scale * (normed_grad - first_mean - normed_local * second_mean)
    gain_term = jnp.sum(scaled_share * normed_local, axis=0)
    back_rows = (packed_grad + cotangent.astype(jnp.float32)).astype(jnp.bfloat16)
    back_padded = jnp.concatenate([back_rows, jnp.zeros((1, quarter), jnp.bfloat16)])
    returning = back_padded[landing.reshape(-1)].reshape(groups, capacity, quarter)
    small_terms = jnp.concatenate([gain_term[None], kernel_term], axis=0)
    small_terms, returning = lax.optimization_barrier((small_terms, returning))
    small_sums = butterfly_sum(small_terms, groups)
    gain_sum, kernel_sum = small_sums[0], small_sums[1:]
    returned = lax.all_to_all(returning, "dp", split_axis=0, concat_axis=0, tiled=True)
    returned_flat = jnp.concatenate(
        [returned.reshape(bucket_slots, quarter), jnp.zeros((1, quarter), jnp.bfloat16)]
    )
    grad_frames = returned_flat[send_pos]
    return (
        output,
        grad_frames,
        gain_sum * inv_root,
        kernel_sum * inv_root,
        grad_expand,
        grad_project,
    )


def solution(mesh):
    placed = (
        P("dp", "seq"),
        P("dp"),
        P("dp", None),
        P(),
        P("dp", None, "seq"),
        P(None, "seq"),
        P("seq", "dp"),
        P("dp", "seq"),
    )
    return jax.shard_map(
        shards,
        mesh=mesh,
        in_specs=placed,
        out_specs=(
            P("dp", "seq"),
            P("dp", "seq"),
            P("seq"),
            P(None, "seq"),
            P("dp", None, "seq"),
            P("seq", "dp"),
        ),
        check_vma=False,
    )
```

```python
import math

import jax
import jax.numpy as jnp
from jax import lax
from jax.sharding import PartitionSpec as P

D = 1536
KSIZE = 9


EPS = 1e-05


def conv_masks(labels):
    half_width = (KSIZE - 1) // 2
    length = labels.shape[0]
    padded = jnp.pad(labels, (half_width, half_width), constant_values=-1)
    return [
        (padded[tap_index : tap_index + length] == labels).astype(jnp.float32)[:, None]
        for tap_index in range(KSIZE)
    ]


def depthwise(signal, kernel, tap_masks):
    half_width = (KSIZE - 1) // 2
    length = signal.shape[0]
    padded = jnp.pad(signal, ((half_width, half_width), (0, 0)))
    total = jnp.zeros(signal.shape, jnp.float32)
    for tap_index in range(KSIZE):
        total = (
            total
            + kernel[tap_index] * padded[tap_index : tap_index + length] * tap_masks[tap_index]
        )
    return total


def depthwise_back(signal, upstream, kernel, tap_masks):
    half_width = (KSIZE - 1) // 2
    length = signal.shape[0]
    padded = jnp.pad(signal, ((half_width, half_width), (0, 0)))
    spread = jnp.zeros((length + 2 * half_width, signal.shape[1]), jnp.float32)
    tap_sums = []
    for tap_index in range(KSIZE):
        masked = upstream * tap_masks[tap_index]
        tap_sums.append(jnp.sum(masked * padded[tap_index : tap_index + length], axis=0))
        spread = spread + jnp.pad(
            kernel[tap_index] * masked, ((tap_index, 2 * half_width - tap_index), (0, 0))
        )
    return (jnp.stack(tap_sums), spread[half_width : half_width + length])


def place_rows(incoming, landing, row_count):
    flat = incoming.reshape(-1, incoming.shape[-1])
    total_slots = flat.shape[0]
    inverse = (
        jnp.full((row_count + 1,), total_slots, jnp.int32)
        .at[landing.reshape(-1)]
        .set(jnp.arange(total_slots, dtype=jnp.int32))[:row_count]
    )
    padded = jnp.concatenate([flat, jnp.zeros((1, flat.shape[1]), flat.dtype)])
    return (padded[inverse], inverse < total_slots)


def dp_bits(groups):
    return groups.bit_length() - 1


def halving_sum(blocks, groups, order, wire=jnp.bfloat16):
    me = lax.axis_index("dp")
    bits = dp_bits(groups)
    rest = blocks.shape[1:]
    cur = blocks.reshape((2,) * bits + rest)
    axis_bits = [bits - 1 - a for a in range(bits)]
    for step, bit in enumerate(order):
        at = axis_bits.index(bit)
        mine = (me >> bit) & 1
        keep = lax.dynamic_index_in_dim(cur, mine, axis=at, keepdims=False)
        send = lax.dynamic_index_in_dim(cur, 1 - mine, axis=at, keepdims=False)
        send = send.astype(wire)
        pairs = [(i, i ^ (1 << bit)) for i in range(groups)]
        cur = keep + lax.ppermute(send, "dp", pairs).astype(keep.dtype)
        axis_bits.pop(at)
    return cur.reshape(rest)


def butterfly_sum(values, groups):
    for bit in range(dp_bits(groups)):
        pairs = [(i, i ^ (1 << bit)) for i in range(groups)]
        values = values + lax.ppermute(values, "dp", pairs)
    return values


def seq_butterfly(values):
    lanes = lax.axis_size("seq")
    for bit in range(lanes.bit_length() - 1):
        pairs = [(i, i ^ (1 << bit)) for i in range(lanes)]
        values = values + lax.ppermute(values, "seq", pairs)
    return values


def doubling_gather(shard, groups, order, wait_for=None, wait_at=0):
    me = lax.axis_index("dp")
    bits = dp_bits(groups)
    cur = shard[None]
    held = []
    for step, bit in enumerate(order):
        if wait_for is not None and step == wait_at:
            cur, _ = lax.optimization_barrier((cur, wait_for))
        pairs = [(i, i ^ (1 << bit)) for i in range(groups)]
        got = lax.ppermute(cur, "dp", pairs)
        low = (me >> bit) & 1 == 0
        cur = jnp.concatenate([jnp.where(low, cur, got), jnp.where(low, got, cur)], axis=0)
        held.insert(0, bit)
    cur = cur.reshape((2,) * bits + shard.shape)
    axes = [held.index(b) for b in reversed(range(bits))]
    cur = jnp.transpose(cur, axes + list(range(bits, bits + shard.ndim)))
    return cur.reshape((groups * shard.shape[0],) + shard.shape[1:])


def link_orders(groups):
    bits = dp_bits(groups)
    z_bits = list(range(1, min(4, bits)))
    y_bits = list(range(4, bits))
    return [0] + z_bits + y_bits, [0] + y_bits + z_bits


def shards(frames, owner_slot, segment, norm_gain, expand, kernel, project, cotangent):
    row_count, quarter = frames.shape
    groups = lax.axis_size("dp")
    lane_index = lax.axis_index("seq")
    capacity = row_count // groups
    bucket_slots = groups * capacity
    dest_group = jnp.where(owner_slot >= 0, owner_slot // row_count, groups)
    onehot = (dest_group[:, None] == jnp.arange(groups, dtype=jnp.int32)[None, :]).astype(jnp.int32)
    earlier = jnp.cumsum(onehot, axis=0) - onehot
    within = jnp.sum(earlier * onehot, axis=1)
    send_pos = jnp.where(owner_slot >= 0, dest_group * capacity + within, bucket_slots)
    source_row = (
        jnp.full((bucket_slots + 1,), row_count, jnp.int32)
        .at[send_pos]
        .set(jnp.arange(row_count, dtype=jnp.int32))[:bucket_slots]
    )
    slot_padded = jnp.concatenate([owner_slot, jnp.full((1,), -1, jnp.int32)])
    named_slot = slot_padded[source_row]
    landing_out = jnp.where(named_slot >= 0, named_slot % row_count, row_count).reshape(
        groups, capacity
    )
    flag_width = 128
    live_flag = jnp.broadcast_to((owner_slot >= 0).astype(jnp.bfloat16)[:, None], (row_count, flag_width))
    padded_in = jnp.concatenate(
        [jnp.concatenate([frames, live_flag], axis=1), jnp.zeros((1, quarter + flag_width), jnp.bfloat16)]
    )
    outgoing = padded_in[source_row].reshape(groups, capacity, quarter + flag_width)
    arrived = lax.all_to_all(outgoing, "dp", split_axis=0, concat_axis=0, tiled=True)
    incoming = arrived[:, :, :quarter]
    sent_count = jnp.sum((arrived[:, :, quarter] > 0.5).astype(jnp.int32), axis=1)
    first_row = jnp.cumsum(sent_count) - sent_count
    slot_rank = jnp.arange(capacity, dtype=jnp.int32)[None, :]
    landing = jnp.where(slot_rank < sent_count[:, None], first_row[:, None] + slot_rank, row_count)
    cot_full = lax.all_gather(cotangent, "seq", axis=1, tiled=True)
    local_rows, occupied = place_rows(incoming, landing, row_count)
    cot_full, local_rows = lax.optimization_barrier((cot_full, local_rows))
    whole_rows = lax.all_gather(local_rows, "seq", axis=1, tiled=True)
    live_col = occupied.astype(jnp.float32)[:, None]
    floats = whole_rows.astype(jnp.float32)
    row_mean = jnp.mean(floats, axis=1, keepdims=True)
    centred = floats - row_mean
    inv_scale = lax.rsqrt(jnp.mean(centred * centred, axis=1, keepdims=True) + EPS)
    normed = centred * inv_scale
    scaled = (normed * norm_gain).astype(jnp.bfloat16)
    z_first, y_first = link_orders(groups)
    block_rows = expand.shape[0]
    both = jnp.concatenate([expand.reshape(block_rows, 2 * quarter), project.T], axis=1)
    both_full = doubling_gather(
        both, groups, z_first[::-1], wait_for=local_rows, wait_at=max(0, dp_bits(groups) - 2)
    )
    expand_full = both_full[:, : 2 * quarter]
    project_full = both_full[:, 2 * quarter :].T
    joined = jnp.dot(scaled, expand_full, preferred_element_type=jnp.float32)
    value_half = joined[:, :quarter]
    gate_sig = jax.nn.sigmoid(joined[:, quarter:])
    glu_out = value_half * gate_sig
    tap_masks = conv_masks(segment[0])
    conv_out = depthwise(glu_out, kernel, tap_masks)
    conv_sig = jax.nn.sigmoid(conv_out)
    hidden = (conv_out * conv_sig * live_col).astype(jnp.bfloat16)
    partial_out = jnp.dot(hidden, project_full, preferred_element_type=jnp.float32)
    mixed_share = lax.psum_scatter(
        partial_out.astype(jnp.bfloat16), "seq", scatter_dimension=1, tiled=True
    ).astype(jnp.float32)
    output = (local_rows.astype(jnp.float32) + mixed_share).astype(jnp.bfloat16)
    inv_root = 1.0 / math.sqrt(row_count * groups)
    project_term = lax.dot_general(
        cot_full, hidden, (((0,), (0,)), ((), ())), preferred_element_type=jnp.float32
    )
    grad_project = (
        halving_sum(project_term.reshape(groups, D // groups, quarter), groups, y_first).T * inv_root
    )
    hidden_grad = (
        lax.dot_general(
            cot_full, project_full, (((1,), (1,)), ((), ())), preferred_element_type=jnp.float32
        )
        * live_col
    )
    conv_grad = hidden_grad * (conv_sig + conv_out * conv_sig * (1.0 - conv_sig))
    kernel_term, glu_grad = depthwise_back(glu_out, conv_grad, kernel, tap_masks)
    proj_grad = jnp.concatenate(
        [glu_grad * gate_sig, glu_grad * value_half * gate_sig * (1.0 - gate_sig)], axis=1
    ).astype(jnp.bfloat16)
    term_block = lax.dot_general(
        scaled, proj_grad, (((0,), (0,)), ((), ())), preferred_element_type=jnp.float32
    )
    grad_expand = (
        halving_sum(term_block.reshape(groups, expand.shape[0], 2, quarter), groups, z_first) * inv_root
    )
    scaled_part = lax.dot_general(
        proj_grad, expand_full, (((1,), (1,)), ((), ())), preferred_element_type=jnp.float32
    )
    normed_local = lax.dynamic_slice_in_dim(normed, lane_index * quarter, quarter, 1)
    gain_local = lax.dynamic_slice_in_dim(norm_gain, lane_index * quarter, quarter, 0)
    scaled_share = lax.psum_scatter(
        scaled_part.astype(jnp.bfloat16), "seq", scatter_dimension=1, tiled=True
    ).astype(jnp.float32)
    normed_grad = scaled_share * gain_local
    row_sums = seq_butterfly(
        jnp.stack([jnp.sum(normed_grad, axis=1), jnp.sum(normed_grad * normed_local, axis=1)])
    )
    first_mean = row_sums[0][:, None] / D
    second_mean = row_sums[1][:, None] / D
    packed_grad = inv_scale * (normed_grad - first_mean - normed_local * second_mean)
    gain_term = jnp.sum(scaled_share * normed_local, axis=0)
    back_rows = (packed_grad + cotangent.astype(jnp.float32)).astype(jnp.bfloat16)
    back_padded = jnp.concatenate([back_rows, jnp.zeros((1, quarter), jnp.bfloat16)])
    returning = back_padded[landing.reshape(-1)].reshape(groups, capacity, quarter)
    small_terms = jnp.concatenate([gain_term[None], kernel_term], axis=0)
    small_terms, returning = lax.optimization_barrier((small_terms, returning))
    small_sums = butterfly_sum(small_terms, groups)
    gain_sum, kernel_sum = small_sums[0], small_sums[1:]
    returned = lax.all_to_all(returning, "dp", split_axis=0, concat_axis=0, tiled=True)
    returned_flat = jnp.concatenate(
        [returned.reshape(bucket_slots, quarter), jnp.zeros((1, quarter), jnp.bfloat16)]
    )
    grad_frames = returned_flat[send_pos]
    return (
        output,
        grad_frames,
        gain_sum * inv_root,
        kernel_sum * inv_root,
        grad_expand,
        grad_project,
    )


def solution(mesh):
    placed = (
        P("dp", "seq"),
        P("dp"),
        P("dp", None),
        P(),
        P("dp", None, "seq"),
        P(None, "seq"),
        P("seq", "dp"),
        P("dp", "seq"),
    )
    return jax.shard_map(
        shards,
        mesh=mesh,
        in_specs=placed,
        out_specs=(
            P("dp", "seq"),
            P("dp", "seq"),
            P("seq"),
            P(None, "seq"),
            P("dp", None, "seq"),
            P("seq", "dp"),
        ),
        check_vma=False,
    )
```
